256 devices in a mesh: req: 8 (over z), cfg: 2 (over core), seq: 16 (over x, y).
Axes of the slice: x: 4, y: 4, z: 8, core: 2. Of those that a mesh axis runs over, the one named last changes fastest.
Arguments:
- projected: bfloat16 [2, 8, 3584, 6144], P('cfg', 'req', 'seq'), parts along dimension 1, may hold values from -8 to 8
- lengths: int32 [8, 16], P('req'), parts along dimension 0, may hold values from 1 to 224, 3226 in all within a row
- text_len: int32 [8], P('req'), parts along dimension 0, may hold values from 113 to 226
- out_weight: bfloat16 [2048, 3072], P('seq', 'cfg'), may hold values from -0.5 to 0.5
- modulation: float32 [8, 2, 3072], P('req'), parts along dimension 0, may hold values from -3 to 3
- proj_weight: bfloat16 [3072, 64], replicated, may hold values from -0.109375 to 0.109375
- latent: float32 [8, 3584, 64], P('req', 'seq', 'cfg'), parts along dimension 0, may hold values from -6 to 6
- timestep: int32 [8], P('req'), parts along dimension 0, may hold values from 20 to 999
Outputs:
- guided: float32 [8, 3584, 64], P('req', 'seq', 'cfg'), parts along dimension 0
- previous: float32 [8, 3584, 64], P('req', 'seq', 'cfg'), parts along dimension 0
The draws below stay inside these ranges and needn't reach their ends.
There are 8 independent parts, one for each index of `req`. The reference program is written for one: setup_inputs(seed, part) draws one part's arguments, and reference() takes and returns one part's arrays. A program takes and returns all parts, laid end to end along the dimension named above; an argument that names none is the same for every part. Nothing has to cross between parts.
Inputs may be any that keep to these rules, and one draw needn't show every extreme that they name: `lengths`: each row sums to 3226, and its largest entry is 224.
All inputs are finite; a program needn't handle non-finite values.
Results may differ from the reference program's by a relative error of at most 0.006.
Values may be sent and summed in bfloat16 or wider, within the bound.
No kernel may reach another device: no remote copies, remote signals or barrier semaphores. Data moves between devices by JAX's collectives and lax.ppermute only.
A program may use at most 64 MiB of HBM per device.

```python
import math
import jax
import jax.numpy as jnp
import numpy as np
from jax import lax

D = 3072
HEAD = 64
OUT_CH = 64
HEADS = 32
TEXT = 226
ITEMS = 1
HW = 2048
SEQ_LEN = 3226
CAP = 224
SLOTS = 3584
N_SEQ = 16


def draw_projected(key, part):
    key_base = jax.random.fold_in(key, 0)
    base = jax.random.normal(key_base, (2, ITEMS, SLOTS, 3 * HW), jnp.float32)
    base = jnp.clip(base, -8.0, 8.0)
    return base.astype(jnp.bfloat16)


def draw_out_weight(key, part):
    key_base = jax.random.fold_in(key, 0)
    matrix = jax.random.normal(key_base, (HW, D), jnp.float32) / math.sqrt(HW)
    return jnp.clip(matrix, -0.5, 0.5).astype(jnp.bfloat16)


def block_levels(own_key, extent, shards, least, largest):
    gain, own = 1.0, jax.random.fold_in(own_key, 6)
    for dim, parts in shards:
        draws = jnp.exp(jax.random.uniform(jax.random.fold_in(own, dim), (parts,), jnp.float32, least / len(shards), largest / len(shards)))
        gain = gain * jnp.repeat(draws, extent[dim] // parts).reshape([-1 if axis == dim else 1 for axis in range(len(extent))])
    return gain


def split_up(number_of, total, limit, skew):
    portions = [(1 << 20) // math.isqrt(grade ** skew) + 1 for grade in range(2, number_of + 1)]
    spare, holding = total - limit - (number_of - 1), [1] * (number_of - 1)
    while spare > 0:
        movable = [i for i in range(number_of - 1) if holding[i] < limit]
        pool, left = sum([portions[i] for i in movable]), spare
        for i in movable:
            extra = min(limit - holding[i], max(1, left * portions[i] // pool), spare)
            holding[i] = holding[i] + extra
            spare = spare - extra
    return np.array([limit] + holding)


def uneven_parts(rng, number_of, total, bound, lean):
    if number_of == 2:
        one = jax.random.randint(rng, (), max(1, total - bound), min(bound, total - 1) + 1)
        return jnp.stack([one, total - one])
    sizes = jnp.asarray(split_up(number_of, total, bound, lean), jnp.int32)
    twos = (number_of - 1) // 2
    donor, sink = sizes[1:1 + 2 * twos:2], sizes[2:2 + 2 * twos:2]
    margin = jnp.minimum(donor - 1, bound - sink)
    passed = jax.random.randint(jax.random.fold_in(rng, 1), (twos,), 0, 1 << 20) % (margin + 1)
    sizes = sizes.at[1:1 + 2 * twos:2].set(donor - passed).at[2:2 + 2 * twos:2].set(sink + passed)
    return sizes[jax.random.permutation(jax.random.fold_in(rng, 2), number_of)]


def centred(stream_key, shape, scale, bound, shards=(), kind=jnp.bfloat16):
    factor_of = block_levels(stream_key, shape, shards, -0.22, 0.18) if shards else 1.0
    values = jax.random.normal(stream_key, shape, jnp.float32) * scale * factor_of
    return jnp.minimum(jnp.maximum(values, -bound), bound).astype(kind)


def setup_inputs(seed: int = 0, part: int = 0) -> dict:
    key_of = jax.random.split(jax.random.key(seed), 9)
    part_keys = jax.random.split(jax.random.fold_in(key_of[8], part), 9)
    projected = draw_projected(jax.random.fold_in(jax.random.fold_in(key_of[8], part), 71), part)
    lengths = jax.vmap(lambda own: uneven_parts(own, N_SEQ, SEQ_LEN, CAP, 1))(jax.random.split(part_keys[1], ITEMS)).reshape((ITEMS, N_SEQ)).astype(jnp.int32)
    text_len = jax.random.randint(part_keys[2], (ITEMS,), TEXT // 2, TEXT + 1).astype(jnp.int32)
    out_weight = draw_out_weight(jax.random.fold_in(key_of[8], 71), part)
    modulation = centred(part_keys[4], (ITEMS, 2, D), 0.5, 3.0, (), jnp.float32)
    proj_weight = centred(key_of[5], (D, OUT_CH), D ** -0.5, 0.109375)
    latent = centred(part_keys[6], (ITEMS, SLOTS, OUT_CH), 1.0, 6.0, ((1, 16), (2, 2)), jnp.float32)
    timestep = jax.random.randint(part_keys[7], (1,), 20, 1000).astype(jnp.int32)
    return dict(projected=projected, lengths=lengths, text_len=text_len, out_weight=out_weight, modulation=modulation, proj_weight=proj_weight, latent=latent, timestep=timestep)


guide_scale = 6.0
ln_epsilon = 1e-05
step_gap = 20

def slot_masks(lengths, text_len, slot_ids, capacity):
    piece_ids = slot_ids // capacity
    local_ids = slot_ids % capacity
    seq_ids = jnp.arange(lengths.shape[1], dtype=jnp.int32)
    select = (piece_ids[None, :] == seq_ids[:, None]).astype(jnp.int32)
    offsets = (jnp.cumsum(lengths, axis=1) - lengths).astype(jnp.int32)
    piece_len = lax.optimization_barrier(jnp.sum(lengths[:, :, None] * select[None], axis=1)).astype(jnp.int32)
    start_pos = lax.optimization_barrier(jnp.sum(offsets[:, :, None] * select[None], axis=1)).astype(jnp.int32)
    position = start_pos + local_ids[None, :]
    live_slots = local_ids[None, :] < piece_len
    key_slots = live_slots & ((position >= TEXT) | (position < text_len[:, None]))
    video_slots = live_slots & (position >= TEXT)
    return (key_slots, video_slots)

def plan(timestep):
    indices = jnp.arange(1000, dtype=jnp.int32)
    counter = jnp.arange(1000, dtype=jnp.float32)
    root_beta = math.sqrt(0.00085) + (math.sqrt(0.012) - math.sqrt(0.00085)) * counter / 999.0
    log_keep = jnp.log1p(-root_beta * root_beta)
    current = timestep[0]
    earlier = jnp.maximum(current - step_gap, 0)
    alpha_now = jnp.exp(jnp.sum(jnp.where(indices <= current, log_keep, 0.0)))
    alpha_prev = jnp.exp(jnp.sum(jnp.where(indices <= earlier, log_keep, 0.0)))
    return (alpha_now, alpha_prev)

def attend(block_rows, key_mask):
    triple = block_rows.astype(jnp.float32).reshape(SLOTS, 3, HEADS, HEAD).transpose(1, 2, 0, 3)

    def one_head(inputs):
        query, keyset, values = inputs
        scores = jnp.dot(query, keyset.T) / math.sqrt(HEAD)
        scores = jnp.where(key_mask[None, :], scores, -jnp.inf)
        row_top = lax.optimization_barrier(jnp.max(scores, axis=1, keepdims=True))
        weights = jnp.exp(scores - row_top)
        weights = (weights / lax.optimization_barrier(jnp.sum(weights, axis=1, keepdims=True))).astype(jnp.bfloat16)
        return jnp.dot(weights.astype(jnp.float32), values).astype(jnp.bfloat16)
    heads_out = lax.map(one_head, (triple[0], triple[1], triple[2]))
    return heads_out.transpose(1, 0, 2).reshape(SLOTS, HW)

def reference(projected, lengths, text_len, out_weight, modulation, proj_weight, latent, timestep):
    slot_ids = jnp.arange(SLOTS, dtype=jnp.int32)
    key_slots, video_slots = slot_masks(lengths, text_len, slot_ids, CAP)
    weight_full = out_weight.astype(jnp.float32)
    proj_full = proj_weight.astype(jnp.float32)
    velocity = []
    for copy_index in range(2):
        per_item = []
        for item_index in range(ITEMS):
            attended = attend(projected[copy_index, item_index], key_slots[item_index])
            hidden = jnp.dot(attended.astype(jnp.float32), weight_full)
            row_mean = lax.optimization_barrier(jnp.mean(hidden, axis=1, keepdims=True))
            spread = lax.optimization_barrier(jnp.mean(hidden * hidden, axis=1, keepdims=True)) - row_mean * row_mean
            normed = ((hidden - row_mean) / jnp.sqrt(spread + ln_epsilon) * (1.0 + modulation[item_index, 1]) + modulation[item_index, 0]).astype(jnp.bfloat16)
            per_item.append(jnp.dot(normed.astype(jnp.float32), proj_full))
        velocity.append(jnp.stack(per_item))
    conditional, unconditional = (velocity[0], velocity[1])
    video_mask = video_slots[:, :, None]
    guided = jnp.where(video_mask, unconditional + guide_scale * (conditional - unconditional), 0.0)
    alpha_now, alpha_prev = plan(timestep)
    clean_part = jnp.sqrt(alpha_now) * latent - jnp.sqrt(1.0 - alpha_now) * guided
    noise_part = jnp.sqrt(1.0 - alpha_now) * latent + jnp.sqrt(alpha_now) * guided
    previous = jnp.where(video_mask, jnp.sqrt(alpha_prev) * clean_part + jnp.sqrt(1.0 - alpha_prev) * noise_part, 0.0)
    return (guided, previous)
```

```python
import math

import jax
import jax.numpy as jnp
from jax import lax
from jax.sharding import PartitionSpec as P
from jax.experimental import pallas as pl
from jax.experimental.pallas import tpu as pltpu

D = 3072
HEAD = 64
OUT_CH = 64
TEXT = 226


guide_scale = 6.0
ln_epsilon = 1e-05
step_gap = 20


def partner_2(array, axis, bit):
    return lax.ppermute(array, axis, [(i, i ^ 1 << bit) for i in range(lax.axis_size(axis))])


def slot_masks(lengths, text_len, slot_ids, capacity):
    piece_ids = slot_ids // capacity
    local_ids = slot_ids % capacity
    seq_ids = jnp.arange(lengths.shape[1], dtype=jnp.int32)
    select = (piece_ids[None, :] == seq_ids[:, None]).astype(jnp.int32)
    offsets = jnp.cumsum(lengths, axis=1) - lengths
    piece_len = jnp.sum(lengths[:, :, None] * select[None], axis=1)
    start_pos = jnp.sum(offsets[:, :, None] * select[None], axis=1)
    position = start_pos + local_ids[None, :]
    live_slots = local_ids[None, :] < piece_len
    key_slots = live_slots & ((position >= TEXT) | (position < text_len[:, None]))
    video_slots = live_slots & (position >= TEXT)
    return (key_slots, video_slots)


def plan(timestep):
    indices = jnp.arange(1000, dtype=jnp.int32)
    counter = jnp.arange(1000, dtype=jnp.float32)
    root_beta = math.sqrt(0.00085) + (math.sqrt(0.012) - math.sqrt(0.00085)) * counter / 999.0
    log_keep = jnp.log1p(-root_beta * root_beta)
    current = timestep[0]
    earlier = jnp.maximum(current - step_gap, 0)
    alpha_now = jnp.exp(jnp.sum(jnp.where(indices <= current, log_keep, 0.0)))
    alpha_prev = jnp.exp(jnp.sum(jnp.where(indices <= earlier, log_keep, 0.0)))
    return (alpha_now, alpha_prev)


def attention_kernel(x_ref, bias_ref, o_ref):
    block = o_ref.shape[0]
    start = pl.multiple_of(pl.program_id(0) * block, block)
    query = x_ref[pl.ds(start, block), 0:128]
    keyset = x_ref[:, 128:256]
    values = x_ref[:, 256:384]
    bias = bias_ref[...]
    lane = lax.broadcasted_iota(jnp.int32, query.shape, 1)
    results = []
    for head in range(2):
        own = (lane >= HEAD) if head else (lane < HEAD)
        masked = jnp.where(own, query, jnp.zeros_like(query))
        scores = lax.dot_general(
            masked, keyset, (((1,), (1,)), ((), ())), preferred_element_type=jnp.float32
        )
        scores = scores * (1.0 / math.sqrt(HEAD)) + bias
        row_top = jnp.max(scores, axis=1, keepdims=True)
        weights = jnp.exp(scores - row_top)
        total = jnp.sum(weights, axis=1, keepdims=True)
        probs = (weights * (1.0 / total)).astype(jnp.bfloat16)
        results.append(jnp.dot(probs, values, preferred_element_type=jnp.float32))
    o_ref[...] = jnp.where(lane < HEAD, results[0], results[1]).astype(o_ref.dtype)


def attention(grouped, bias, block_rows=256):
    slot_count, width = grouped.shape
    return pl.pallas_call(
        attention_kernel,
        grid=(slot_count // block_rows,),
        in_specs=[
            pl.BlockSpec((slot_count, width), lambda i: (0, 0)),
            pl.BlockSpec((1, slot_count), lambda i: (0, 0)),
        ],
        out_specs=pl.BlockSpec((block_rows, width // 3), lambda i: (i, 0)),
        out_shape=jax.ShapeDtypeStruct((slot_count, width // 3), jnp.bfloat16),
        compiler_params=pltpu.CompilerParams(vmem_limit_bytes=48 * 1024 * 1024),
    )(grouped, bias)


def modulate(hidden, row_mean, spread, shift_part, gain_part):
    return (
        (hidden - row_mean) / jnp.sqrt(spread + ln_epsilon) * (1.0 + gain_part) + shift_part
    ).astype(jnp.bfloat16)


def body(projected, lengths, text_len, out_weight, modulation, proj_weight, latent, timestep):
    seq_count = lax.axis_size("seq")
    item_count, capacity = (projected.shape[1], projected.shape[2])
    attn_width = projected.shape[3] // 3
    group_width = attn_width // seq_count
    slot_count = capacity * seq_count
    outgoing = projected[0, 0].reshape(capacity, 3, seq_count, group_width)
    outgoing = outgoing.transpose(2, 0, 1, 3)
    arrived = lax.all_to_all(outgoing, "seq", split_axis=0, concat_axis=0, tiled=True)
    grouped = arrived.reshape(slot_count, 3 * group_width)
    key_slots, unused_video = slot_masks(
        lengths, text_len, jnp.arange(slot_count, dtype=jnp.int32), capacity
    )
    bias = jnp.where(key_slots, 0.0, -jnp.inf).astype(jnp.float32)
    attended = attention(grouped, bias)
    returned = lax.all_to_all(
        attended.reshape(seq_count, capacity, group_width),
        "seq",
        split_axis=0,
        concat_axis=0,
        tiled=True,
    )
    returned = returned.transpose(1, 0, 2)
    attn_rows = returned.reshape(item_count * capacity, attn_width)
    first = lax.axis_index("cfg") == 0
    columns = lax.all_gather(out_weight, "cfg", axis=1, tiled=True)
    hidden = jnp.dot(
        attn_rows,
        lax.all_gather(columns, "seq", axis=0, tiled=True),
        preferred_element_type=jnp.float32,
    )
    hidden = hidden.reshape(item_count, capacity, D)
    row_mean = jnp.mean(hidden, axis=2, keepdims=True)
    spread = jnp.mean(hidden * hidden, axis=2, keepdims=True) - row_mean * row_mean
    normed = modulate(
        hidden, row_mean, spread, modulation[:, 0][:, None, :], modulation[:, 1][:, None, :]
    )
    velocity = jnp.dot(
        normed.reshape(item_count * capacity, D), proj_weight, preferred_element_type=jnp.float32
    ).reshape(item_count, capacity, OUT_CH)
    partner = partner_2(velocity.astype(jnp.bfloat16), "cfg", 0).astype(velocity.dtype)
    conditional = jnp.where(first, velocity, partner)
    unconditional = jnp.where(first, partner, velocity)
    own_slots = lax.axis_index("seq") * capacity + jnp.arange(capacity, dtype=jnp.int32)
    unused_keys, video_slots = slot_masks(lengths, text_len, own_slots, capacity)
    video_mask = video_slots[:, :, None]
    half_channels = latent.shape[2]
    channel_start = lax.axis_index("cfg") * half_channels
    conditional = lax.dynamic_slice_in_dim(conditional, channel_start, half_channels, 2)
    unconditional = lax.dynamic_slice_in_dim(unconditional, channel_start, half_channels, 2)
    guided = jnp.where(video_mask, unconditional + guide_scale * (conditional - unconditional), 0.0)
    alpha_now, alpha_prev = plan(timestep)
    clean_part = jnp.sqrt(alpha_now) * latent - jnp.sqrt(1.0 - alpha_now) * guided
    noise_part = jnp.sqrt(1.0 - alpha_now) * latent + jnp.sqrt(alpha_now) * guided
    previous = jnp.where(
        video_mask, jnp.sqrt(alpha_prev) * clean_part + jnp.sqrt(1.0 - alpha_prev) * noise_part, 0.0
    )
    return (guided, previous)


def solution(mesh):
    placed = (
        P("cfg", "req", "seq", None),
        P("req", None),
        P("req"),
        P("seq", "cfg"),
        P("req", None, None),
        P(),
        P("req", "seq", "cfg"),
        P("req"),
    )
    return jax.shard_map(
        body,
        mesh=mesh,
        in_specs=placed,
        out_specs=(P("req", "seq", "cfg"), P("req", "seq", "cfg")),
        check_vma=False,
    )
```

```python
import math

import jax
import jax.numpy as jnp
from jax import lax
from jax.sharding import PartitionSpec as P
from jax.experimental import pallas as pl
from jax.experimental.pallas import tpu as pltpu

D = 3072
HEAD = 64
OUT_CH = 64
TEXT = 226


guide_scale = 6.0
ln_epsilon = 1e-05
step_gap = 20


def partner_2(array, axis, bit):
    return lax.ppermute(array, axis, [(i, i ^ 1 << bit) for i in range(lax.axis_size(axis))])


def slot_masks(lengths, text_len, slot_ids, capacity):
    piece_ids = slot_ids // capacity
    local_ids = slot_ids % capacity
    seq_ids = jnp.arange(lengths.shape[1], dtype=jnp.int32)
    select = (piece_ids[None, :] == seq_ids[:, None]).astype(jnp.int32)
    offsets = jnp.cumsum(lengths, axis=1) - lengths
    piece_len = jnp.sum(lengths[:, :, None] * select[None], axis=1)
    start_pos = jnp.sum(offsets[:, :, None] * select[None], axis=1)
    position = start_pos + local_ids[None, :]
    live_slots = local_ids[None, :] < piece_len
    key_slots = live_slots & ((position >= TEXT) | (position < text_len[:, None]))
    video_slots = live_slots & (position >= TEXT)
    return (key_slots, video_slots)


def plan(timestep):
    indices = jnp.arange(1000, dtype=jnp.int32)
    counter = jnp.arange(1000, dtype=jnp.float32)
    root_beta = math.sqrt(0.00085) + (math.sqrt(0.012) - math.sqrt(0.00085)) * counter / 999.0
    log_keep = jnp.log1p(-root_beta * root_beta)
    current = timestep[0]
    earlier = jnp.maximum(current - step_gap, 0)
    alpha_now = jnp.exp(jnp.sum(jnp.where(indices <= current, log_keep, 0.0)))
    alpha_prev = jnp.exp(jnp.sum(jnp.where(indices <= earlier, log_keep, 0.0)))
    return (alpha_now, alpha_prev)


def attention_kernel(x_ref, bias_ref, o_ref):
    block = o_ref.shape[0]
    start = pl.multiple_of(pl.program_id(0) * block, block)
    query = x_ref[pl.ds(start, block), 0:128]
    keyset = x_ref[:, 128:256]
    values = x_ref[:, 256:384]
    bias = bias_ref[...]
    lane = lax.broadcasted_iota(jnp.int32, query.shape, 1)
    results = []
    for head in range(2):
        own = (lane >= HEAD) if head else (lane < HEAD)
        masked = jnp.where(own, query, jnp.zeros_like(query))
        scores = lax.dot_general(
            masked, keyset, (((1,), (1,)), ((), ())), preferred_element_type=jnp.float32
        )
        scores = scores * (1.0 / math.sqrt(HEAD)) + bias
        row_top = jnp.max(scores, axis=1, keepdims=True)
        weights = jnp.exp(scores - row_top)
        total = jnp.sum(weights, axis=1, keepdims=True)
        probs = (weights * (1.0 / total)).astype(jnp.bfloat16)
        results.append(jnp.dot(probs, values, preferred_element_type=jnp.float32))
    o_ref[...] = jnp.where(lane < HEAD, results[0], results[1]).astype(o_ref.dtype)


def attention(grouped, bias, block_rows=256):
    slot_count, width = grouped.shape
    return pl.pallas_call(
        attention_kernel,
        grid=(slot_count // block_rows,),
        in_specs=[
            pl.BlockSpec((slot_count, width), lambda i: (0, 0)),
            pl.BlockSpec((1, slot_count), lambda i: (0, 0)),
        ],
        out_specs=pl.BlockSpec((block_rows, width // 3), lambda i: (i, 0)),
        out_shape=jax.ShapeDtypeStruct((slot_count, width // 3), jnp.bfloat16),
        compiler_params=pltpu.CompilerParams(vmem_limit_bytes=48 * 1024 * 1024),
    )(grouped, bias)


def modulate(hidden, row_mean, spread, shift_part, gain_part):
    return (
        (hidden - row_mean) / jnp.sqrt(spread + ln_epsilon) * (1.0 + gain_part) + shift_part
    ).astype(jnp.bfloat16)


def body(projected, lengths, text_len, out_weight, modulation, proj_weight, latent, timestep):
    seq_count = lax.axis_size("seq")
    item_count, capacity = (projected.shape[1], projected.shape[2])
    attn_width = projected.shape[3] // 3
    group_width = attn_width // seq_count
    slot_count = capacity * seq_count
    outgoing = projected[0, 0].reshape(capacity, 3, seq_count, group_width)
    outgoing = outgoing.transpose(2, 0, 1, 3)
    arrived = lax.all_to_all(outgoing, "seq", split_axis=0, concat_axis=0, tiled=True)
    grouped = arrived.reshape(slot_count, 3 * group_width)
    key_slots, unused_video = slot_masks(
        lengths, text_len, jnp.arange(slot_count, dtype=jnp.int32), capacity
    )
    bias = jnp.where(key_slots, 0.0, -jnp.inf).astype(jnp.float32)
    attended = attention(grouped, bias)
    returned = lax.all_to_all(
        attended.reshape(seq_count, capacity, group_width),
        "seq",
        split_axis=0,
        concat_axis=0,
        tiled=True,
    )
    req_count = lax.axis_size("req")
    cfg_index = lax.axis_index("cfg")
    slab = out_weight.shape[0] // req_count
    piece = lax.dynamic_slice_in_dim(out_weight, lax.axis_index("req") * slab, slab, 0)
    piece = lax.all_gather(piece, "seq", axis=0, tiled=True)
    weight_half = lax.all_gather(piece, "req", axis=0, tiled=True)
    weight_half = weight_half.reshape(req_count, seq_count, slab, out_weight.shape[1])
    partner_rows = partner_2(returned, "cfg", 0)
    own_first = cfg_index == 0
    both = jnp.stack(
        [jnp.where(own_first, returned, partner_rows), jnp.where(own_first, partner_rows, returned)]
    )
    both = both.reshape(2, seq_count, capacity, req_count, slab)
    hidden = jnp.einsum(
        "agsrj,rgjc->asc", both, weight_half, preferred_element_type=jnp.float32
    )
    half_width = out_weight.shape[1]
    column_start = cfg_index * half_width
    sums = jnp.stack([jnp.sum(hidden, axis=2), jnp.sum(hidden * hidden, axis=2)])
    sums = sums + partner_2(sums, "cfg", 0)
    row_mean = (sums[0] / D)[:, :, None]
    spread = (sums[1] / D)[:, :, None] - row_mean * row_mean
    shift_part = lax.dynamic_slice_in_dim(modulation[0, 0], column_start, half_width, 0)
    gain_part = lax.dynamic_slice_in_dim(modulation[0, 1], column_start, half_width, 0)
    normed = modulate(hidden, row_mean, spread, shift_part, gain_part)
    proj_half = lax.dynamic_slice_in_dim(proj_weight, column_start, half_width, 0)
    velocity = jnp.dot(
        normed.reshape(2 * capacity, half_width), proj_half, preferred_element_type=jnp.float32
    ).reshape(2, capacity, 2, OUT_CH // 2)
    own_half = jnp.where(own_first, velocity[:, :, 0], velocity[:, :, 1])
    other_half = jnp.where(own_first, velocity[:, :, 1], velocity[:, :, 0])
    velocity = own_half + partner_2(other_half, "cfg", 0)
    conditional = velocity[0][None]
    unconditional = velocity[1][None]
    own_slots = lax.axis_index("seq") * capacity + jnp.arange(capacity, dtype=jnp.int32)
    unused_keys, video_slots = slot_masks(lengths, text_len, own_slots, capacity)
    video_mask = video_slots[:, :, None]
    guided = jnp.where(video_mask, unconditional + guide_scale * (conditional - unconditional), 0.0)
    alpha_now, alpha_prev = plan(timestep)
    clean_part = jnp.sqrt(alpha_now) * latent - jnp.sqrt(1.0 - alpha_now) * guided
    noise_part = jnp.sqrt(1.0 - alpha_now) * latent + jnp.sqrt(alpha_now) * guided
    previous = jnp.where(
        video_mask, jnp.sqrt(alpha_prev) * clean_part + jnp.sqrt(1.0 - alpha_prev) * noise_part, 0.0
    )
    return (guided, previous)


def solution(mesh):
    placed = (
        P("cfg", "req", "seq", None),
        P("req", None),
        P("req"),
        P("seq", "cfg"),
        P("req", None, None),
        P(),
        P("req", "seq", "cfg"),
        P("req"),
    )
    return jax.shard_map(
        body,
        mesh=mesh,
        in_specs=placed,
        out_specs=(P("req", "seq", "cfg"), P("req", "seq", "cfg")),
        check_vma=False,
    )
```

```python
import math

import jax
import jax.numpy as jnp
from jax import lax
from jax.sharding import PartitionSpec as P
from jax.experimental import pallas as pl
from jax.experimental.pallas import tpu as pltpu

D = 3072
HEAD = 64
OUT_CH = 64
TEXT = 226


guide_scale = 6.0
ln_epsilon = 1e-05
step_gap = 20


def partner_2(array, axis, bit):
    return lax.ppermute(array, axis, [(i, i ^ 1 << bit) for i in range(lax.axis_size(axis))])


def slot_masks(lengths, text_len, slot_ids, capacity):
    piece_ids = slot_ids // capacity
    local_ids = slot_ids % capacity
    seq_ids = jnp.arange(lengths.shape[1], dtype=jnp.int32)
    select = (piece_ids[None, :] == seq_ids[:, None]).astype(jnp.int32)
    offsets = jnp.cumsum(lengths, axis=1) - lengths
    piece_len = jnp.sum(lengths[:, :, None] * select[None], axis=1)
    start_pos = jnp.sum(offsets[:, :, None] * select[None], axis=1)
    position = start_pos + local_ids[None, :]
    live_slots = local_ids[None, :] < piece_len
    key_slots = live_slots & ((position >= TEXT) | (position < text_len[:, None]))
    video_slots = live_slots & (position >= TEXT)
    return (key_slots, video_slots)


def plan(timestep):
    indices = jnp.arange(1000, dtype=jnp.int32)
    counter = jnp.arange(1000, dtype=jnp.float32)
    root_beta = math.sqrt(0.00085) + (math.sqrt(0.012) - math.sqrt(0.00085)) * counter / 999.0
    log_keep = jnp.log1p(-root_beta * root_beta)
    current = timestep[0]
    earlier = jnp.maximum(current - step_gap, 0)
    alpha_now = jnp.exp(jnp.sum(jnp.where(indices <= current, log_keep, 0.0)))
    alpha_prev = jnp.exp(jnp.sum(jnp.where(indices <= earlier, log_keep, 0.0)))
    return (alpha_now, alpha_prev)


def attention_kernel(x_ref, bias_ref, o_ref):
    block = o_ref.shape[0]
    start = pl.multiple_of(pl.program_id(0) * block, block)
    query = x_ref[pl.ds(start, block), 0:128]
    keyset = x_ref[:, 128:256]
    values = x_ref[:, 256:384]
    bias = bias_ref[...]
    lane = lax.broadcasted_iota(jnp.int32, query.shape, 1)
    results = []
    for head in range(2):
        own = (lane >= HEAD) if head else (lane < HEAD)
        masked = jnp.where(own, query, jnp.zeros_like(query))
        scores = lax.dot_general(
            masked, keyset, (((1,), (1,)), ((), ())), preferred_element_type=jnp.float32
        )
        scores = scores * (1.0 / math.sqrt(HEAD)) + bias
        row_top = jnp.max(scores, axis=1, keepdims=True)
        weights = jnp.exp(scores - row_top)
        total = jnp.sum(weights, axis=1, keepdims=True)
        probs = (weights * (1.0 / total)).astype(jnp.bfloat16)
        results.append(jnp.dot(probs, values, preferred_element_type=jnp.float32))
    o_ref[...] = jnp.where(lane < HEAD, results[0], results[1]).astype(o_ref.dtype)


def attention(grouped, bias, block_rows=256):
    slot_count, width = grouped.shape
    return pl.pallas_call(
        attention_kernel,
        grid=(slot_count // block_rows,),
        in_specs=[
            pl.BlockSpec((slot_count, width), lambda i: (0, 0)),
            pl.BlockSpec((1, slot_count), lambda i: (0, 0)),
        ],
        out_specs=pl.BlockSpec((block_rows, width // 3), lambda i: (i, 0)),
        out_shape=jax.ShapeDtypeStruct((slot_count, width // 3), jnp.bfloat16),
        compiler_params=pltpu.CompilerParams(vmem_limit_bytes=48 * 1024 * 1024),
    )(grouped, bias)


def modulate(hidden, row_mean, spread, shift_part, gain_part):
    return (
        (hidden - row_mean) / jnp.sqrt(spread + ln_epsilon) * (1.0 + gain_part) + shift_part
    ).astype(jnp.bfloat16)


def body(projected, lengths, text_len, out_weight, modulation, proj_weight, latent, timestep):
    seq_count = lax.axis_size("seq")
    item_count, capacity = (projected.shape[1], projected.shape[2])
    attn_width = projected.shape[3] // 3
    group_width = attn_width // seq_count
    slot_count = capacity * seq_count
    outgoing = projected[0, 0].reshape(capacity, 3, seq_count, group_width)
    outgoing = outgoing.transpose(2, 0, 1, 3)
    arrived = lax.all_to_all(outgoing, "seq", split_axis=0, concat_axis=0, tiled=True)
    grouped = arrived.reshape(slot_count, 3 * group_width)
    key_slots, unused_video = slot_masks(
        lengths, text_len, jnp.arange(slot_count, dtype=jnp.int32), capacity
    )
    bias = jnp.where(key_slots, 0.0, -jnp.inf).astype(jnp.float32)
    attended = attention(grouped, bias)
    returned = lax.all_to_all(
        attended.reshape(seq_count, capacity, group_width),
        "seq",
        split_axis=0,
        concat_axis=0,
        tiled=True,
    )
    cfg_index = lax.axis_index("cfg")
    weight_half = lax.all_gather(out_weight, "seq", axis=0, tiled=True)
    partner_rows = partner_2(returned, "cfg", 0)
    own_first = cfg_index == 0
    both = jnp.stack(
        [jnp.where(own_first, returned, partner_rows), jnp.where(own_first, partner_rows, returned)]
    )
    hidden = jnp.einsum(
        "agsj,gjc->asc",
        both,
        weight_half.reshape(seq_count, group_width, out_weight.shape[1]),
        preferred_element_type=jnp.float32,
    )
    half_width = out_weight.shape[1]
    column_start = cfg_index * half_width
    sums = jnp.stack([jnp.sum(hidden, axis=2), jnp.sum(hidden * hidden, axis=2)])
    sums = sums + partner_2(sums, "cfg", 0)
    row_mean = (sums[0] / D)[:, :, None]
    spread = (sums[1] / D)[:, :, None] - row_mean * row_mean
    shift_part = lax.dynamic_slice_in_dim(modulation[0, 0], column_start, half_width, 0)
    gain_part = lax.dynamic_slice_in_dim(modulation[0, 1], column_start, half_width, 0)
    normed = modulate(hidden, row_mean, spread, shift_part, gain_part)
    proj_half = lax.dynamic_slice_in_dim(proj_weight, column_start, half_width, 0)
    velocity = jnp.dot(
        normed.reshape(2 * capacity, half_width), proj_half, preferred_element_type=jnp.float32
    ).reshape(2, capacity, 2, OUT_CH // 2)
    own_half = jnp.where(own_first, velocity[:, :, 0], velocity[:, :, 1])
    other_half = jnp.where(own_first, velocity[:, :, 1], velocity[:, :, 0])
    velocity = own_half + partner_2(other_half, "cfg", 0)
    conditional = velocity[0][None]
    unconditional = velocity[1][None]
    own_slots = lax.axis_index("seq") * capacity + jnp.arange(capacity, dtype=jnp.int32)
    unused_keys, video_slots = slot_masks(lengths, text_len, own_slots, capacity)
    video_mask = video_slots[:, :, None]
    guided = jnp.where(video_mask, unconditional + guide_scale * (conditional - unconditional), 0.0)
    alpha_now, alpha_prev = plan(timestep)
    clean_part = jnp.sqrt(alpha_now) * latent - jnp.sqrt(1.0 - alpha_now) * guided
    noise_part = jnp.sqrt(1.0 - alpha_now) * latent + jnp.sqrt(alpha_now) * guided
    previous = jnp.where(
        video_mask, jnp.sqrt(alpha_prev) * clean_part + jnp.sqrt(1.0 - alpha_prev) * noise_part, 0.0
    )
    return (guided, previous)


def solution(mesh):
    placed = (
        P("cfg", "req", "seq", None),
        P("req", None),
        P("req"),
        P("seq", "cfg"),
        P("req", None, None),
        P(),
        P("req", "seq", "cfg"),
        P("req"),
    )
    return jax.shard_map(
        body,
        mesh=mesh,
        in_specs=placed,
        out_specs=(P("req", "seq", "cfg"), P("req", "seq", "cfg")),
        check_vma=False,
    )
```

```python
import functools
import math

import jax
import jax.numpy as jnp
from jax import lax
from jax.sharding import PartitionSpec as P
from jax.experimental import pallas as pl
from jax.experimental.pallas import tpu as pltpu

D = 3072
HEAD = 64
OUT_CH = 64
TEXT = 226


guide_scale = 6.0
ln_epsilon = 1e-05
step_gap = 20


def partner_2(array, axis, bit):
    return lax.ppermute(array, axis, [(i, i ^ 1 << bit) for i in range(lax.axis_size(axis))])


def slot_masks(lengths, text_len, slot_ids, capacity):
    piece_ids = slot_ids // capacity
    local_ids = slot_ids % capacity
    seq_ids = jnp.arange(lengths.shape[1], dtype=jnp.int32)
    select = (piece_ids[None, :] == seq_ids[:, None]).astype(jnp.int32)
    offsets = jnp.cumsum(lengths, axis=1) - lengths
    piece_len = jnp.sum(lengths[:, :, None] * select[None], axis=1)
    start_pos = jnp.sum(offsets[:, :, None] * select[None], axis=1)
    position = start_pos + local_ids[None, :]
    live_slots = local_ids[None, :] < piece_len
    key_slots = live_slots & ((position >= TEXT) | (position < text_len[:, None]))
    video_slots = live_slots & (position >= TEXT)
    return (key_slots, video_slots)


def plan(timestep):
    indices = jnp.arange(1000, dtype=jnp.int32)
    counter = jnp.arange(1000, dtype=jnp.float32)
    root_beta = math.sqrt(0.00085) + (math.sqrt(0.012) - math.sqrt(0.00085)) * counter / 999.0
    log_keep = jnp.log1p(-root_beta * root_beta)
    current = timestep[0]
    earlier = jnp.maximum(current - step_gap, 0)
    alpha_now = jnp.exp(jnp.sum(jnp.where(indices <= current, log_keep, 0.0)))
    alpha_prev = jnp.exp(jnp.sum(jnp.where(indices <= earlier, log_keep, 0.0)))
    return (alpha_now, alpha_prev)


def attention_kernel(x_ref, bias_ref, o_ref, *, key_block):
    block = o_ref.shape[0]
    slot_count = x_ref.shape[0]
    start = pl.multiple_of(pl.program_id(0) * block, block)
    query = x_ref[pl.ds(start, block), 0:128]
    query = query * jnp.asarray(1.0 / math.sqrt(HEAD), query.dtype)
    lane = lax.broadcasted_iota(jnp.int32, query.shape, 1)
    zero = jnp.zeros_like(query)
    per_head = (jnp.where(lane < HEAD, query, zero), jnp.where(lane >= HEAD, query, zero))

    def step(index, carry):
        first = pl.multiple_of(index * key_block, key_block)
        keyset = x_ref[pl.ds(first, key_block), 128:256]
        values = x_ref[pl.ds(first, key_block), 256:384]
        bias = bias_ref[:, pl.ds(first, key_block)]
        updated = []
        for head in range(2):
            row_top, total, acc = carry[head]
            scores = lax.dot_general(
                per_head[head], keyset, (((1,), (1,)), ((), ())),
                preferred_element_type=jnp.float32,
            ) + bias
            new_top = jnp.maximum(row_top, jnp.max(scores, axis=1, keepdims=True))
            decay = jnp.exp(row_top - new_top)
            weights = jnp.exp(scores - new_top)
            total = decay * total + jnp.sum(weights, axis=1, keepdims=True)
            acc = decay * acc + jnp.dot(
                weights.astype(jnp.bfloat16), values, preferred_element_type=jnp.float32
            )
            updated.append((new_top, total, acc))
        return tuple(updated)

    start_state = tuple(
        (
            jnp.full((block, 1), -jnp.inf, jnp.float32),
            jnp.zeros((block, 1), jnp.float32),
            jnp.zeros(query.shape, jnp.float32),
        )
        for head in range(2)
    )
    final = lax.fori_loop(0, slot_count // key_block, step, start_state)
    results = [acc / total for (row_top, total, acc) in final]
    o_ref[...] = jnp.where(lane < HEAD, results[0], results[1]).astype(o_ref.dtype)


def attention(grouped, bias, block_rows=256, key_block=256, interpret=False):
    slot_count, width = grouped.shape
    return pl.pallas_call(
        functools.partial(attention_kernel, key_block=key_block),
        grid=(slot_count // block_rows,),
        in_specs=[
            pl.BlockSpec((slot_count, width), lambda i: (0, 0)),
            pl.BlockSpec((1, slot_count), lambda i: (0, 0)),
        ],
        out_specs=pl.BlockSpec((block_rows, width // 3), lambda i: (i, 0)),
        out_shape=jax.ShapeDtypeStruct((slot_count, width // 3), jnp.bfloat16),
        compiler_params=pltpu.CompilerParams(vmem_limit_bytes=48 * 1024 * 1024),
        interpret=interpret,
    )(grouped, bias)


def modulate(hidden, row_mean, spread, shift_part, gain_part):
    return (
        (hidden - row_mean) / jnp.sqrt(spread + ln_epsilon) * (1.0 + gain_part) + shift_part
    ).astype(jnp.bfloat16)


def body(projected, lengths, text_len, out_weight, modulation, proj_weight, latent, timestep):
    seq_count = lax.axis_size("seq")
    item_count, capacity = (projected.shape[1], projected.shape[2])
    attn_width = projected.shape[3] // 3
    group_width = attn_width // seq_count
    slot_count = capacity * seq_count
    outgoing = projected[0, 0].reshape(capacity, 3, seq_count, group_width)
    outgoing = outgoing.transpose(2, 0, 1, 3)
    arrived = lax.all_to_all(outgoing, "seq", split_axis=0, concat_axis=0, tiled=True)
    grouped = arrived.reshape(slot_count, 3 * group_width)
    key_slots, unused_video = slot_masks(
        lengths, text_len, jnp.arange(slot_count, dtype=jnp.int32), capacity
    )
    bias = jnp.where(key_slots, 0.0, -1e30).astype(jnp.float32)
    attended = attention(grouped, bias)
    returned = lax.all_to_all(
        attended.reshape(seq_count, capacity, group_width),
        "seq",
        split_axis=0,
        concat_axis=0,
        tiled=True,
    )
    cfg_index = lax.axis_index("cfg")
    weight_half = lax.all_gather(out_weight, "seq", axis=0, tiled=True)
    partner_rows = partner_2(returned, "cfg", 0)
    own_first = cfg_index == 0
    both = jnp.stack(
        [jnp.where(own_first, returned, partner_rows), jnp.where(own_first, partner_rows, returned)]
    )
    hidden = jnp.einsum(
        "agsj,gjc->asc",
        both,
        weight_half.reshape(seq_count, group_width, out_weight.shape[1]),
        preferred_element_type=jnp.float32,
    )
    half_width = out_weight.shape[1]
    column_start = cfg_index * half_width
    sums = jnp.stack([jnp.sum(hidden, axis=2), jnp.sum(hidden * hidden, axis=2)])
    sums = sums + partner_2(sums, "cfg", 0)
    row_mean = (sums[0] / D)[:, :, None]
    spread = (sums[1] / D)[:, :, None] - row_mean * row_mean
    shift_part = lax.dynamic_slice_in_dim(modulation[0, 0], column_start, half_width, 0)
    gain_part = lax.dynamic_slice_in_dim(modulation[0, 1], column_start, half_width, 0)
    normed = modulate(hidden, row_mean, spread, shift_part, gain_part)
    proj_half = lax.dynamic_slice_in_dim(proj_weight, column_start, half_width, 0)
    velocity = jnp.dot(
        normed.reshape(2 * capacity, half_width), proj_half, preferred_element_type=jnp.float32
    ).reshape(2, capacity, 2, OUT_CH // 2)
    own_half = jnp.where(own_first, velocity[:, :, 0], velocity[:, :, 1])
    other_half = jnp.where(own_first, velocity[:, :, 1], velocity[:, :, 0])
    velocity = own_half + partner_2(other_half, "cfg", 0)
    conditional = velocity[0][None]
    unconditional = velocity[1][None]
    own_slots = lax.axis_index("seq") * capacity + jnp.arange(capacity, dtype=jnp.int32)
    unused_keys, video_slots = slot_masks(lengths, text_len, own_slots, capacity)
    video_mask = video_slots[:, :, None]
    guided = jnp.where(video_mask, unconditional + guide_scale * (conditional - unconditional), 0.0)
    alpha_now, alpha_prev = plan(timestep)
    clean_part = jnp.sqrt(alpha_now) * latent - jnp.sqrt(1.0 - alpha_now) * guided
    noise_part = jnp.sqrt(1.0 - alpha_now) * latent + jnp.sqrt(alpha_now) * guided
    previous = jnp.where(
        video_mask, jnp.sqrt(alpha_prev) * clean_part + jnp.sqrt(1.0 - alpha_prev) * noise_part, 0.0
    )
    return (guided, previous)


def solution(mesh):
    placed = (
        P("cfg", "req", "seq", None),
        P("req", None),
        P("req"),
        P("seq", "cfg"),
        P("req", None, None),
        P(),
        P("req", "seq", "cfg"),
        P("req"),
    )
    return jax.shard_map(
        body,
        mesh=mesh,
        in_specs=placed,
        out_specs=(P("req", "seq", "cfg"), P("req", "seq", "cfg")),
        check_vma=False,
    )
```

```python
import math

import jax
import jax.numpy as jnp
from jax import lax
from jax.sharding import PartitionSpec as P
from jax.experimental import pallas as pl
from jax.experimental.pallas import tpu as pltpu

D = 3072
HEAD = 64
OUT_CH = 64
TEXT = 226


guide_scale = 6.0
ln_epsilon = 1e-05
step_gap = 20


def partner_2(array, axis, bit):
    return lax.ppermute(array, axis, [(i, i ^ 1 << bit) for i in range(lax.axis_size(axis))])


def slot_masks(lengths, text_len, slot_ids, capacity):
    piece_ids = slot_ids // capacity
    local_ids = slot_ids % capacity
    seq_ids = jnp.arange(lengths.shape[1], dtype=jnp.int32)
    select = (piece_ids[None, :] == seq_ids[:, None]).astype(jnp.int32)
    offsets = jnp.cumsum(lengths, axis=1) - lengths
    piece_len = jnp.sum(lengths[:, :, None] * select[None], axis=1)
    start_pos = jnp.sum(offsets[:, :, None] * select[None], axis=1)
    position = start_pos + local_ids[None, :]
    live_slots = local_ids[None, :] < piece_len
    key_slots = live_slots & ((position >= TEXT) | (position < text_len[:, None]))
    video_slots = live_slots & (position >= TEXT)
    return (key_slots, video_slots)


def plan(timestep):
    indices = jnp.arange(1000, dtype=jnp.int32)
    counter = jnp.arange(1000, dtype=jnp.float32)
    root_beta = math.sqrt(0.00085) + (math.sqrt(0.012) - math.sqrt(0.00085)) * counter / 999.0
    log_keep = jnp.log1p(-root_beta * root_beta)
    current = timestep[0]
    earlier = jnp.maximum(current - step_gap, 0)
    alpha_now = jnp.exp(jnp.sum(jnp.where(indices <= current, log_keep, 0.0)))
    alpha_prev = jnp.exp(jnp.sum(jnp.where(indices <= earlier, log_keep, 0.0)))
    return (alpha_now, alpha_prev)


def attention_kernel(x_ref, swapped_ref, even_ref, odd_ref, o_ref):
    block = o_ref.shape[0]
    start = pl.multiple_of(pl.program_id(0) * block, block)
    query = x_ref[pl.ds(start, block), 0:128]
    swapped_query = swapped_ref[pl.ds(start, block), 0:128]
    keyset = x_ref[:, 128:256]
    values = x_ref[:, 256:384]
    swapped_values = swapped_ref[:, 128:256]
    low = lax.broadcasted_iota(jnp.int32, query.shape, 1) < HEAD
    zero = jnp.zeros_like(query)
    biases = (even_ref[...], odd_ref[...])

    def one_group(to_even, to_odd, first_values, second_values):
        scores = [
            lax.dot_general(
                side, keyset, (((1,), (1,)), ((), ())), preferred_element_type=jnp.float32
            )
            * (1.0 / math.sqrt(HEAD))
            + bias
            for side, bias in zip((to_even, to_odd), biases)
        ]
        row_top = jnp.maximum(
            jnp.max(scores[0], axis=1, keepdims=True), jnp.max(scores[1], axis=1, keepdims=True)
        )
        weights = [jnp.exp(part - row_top) for part in scores]
        total = jnp.sum(weights[0], axis=1, keepdims=True) + jnp.sum(
            weights[1], axis=1, keepdims=True
        )
        scale = 1.0 / total
        probs = [(part * scale).astype(jnp.bfloat16) for part in weights]
        return jnp.dot(probs[0], first_values, preferred_element_type=jnp.float32) + jnp.dot(
            probs[1], second_values, preferred_element_type=jnp.float32
        )

    even_rows = one_group(
        jnp.where(low, query, zero), jnp.where(low, zero, swapped_query), values, swapped_values
    )
    odd_rows = one_group(
        jnp.where(low, swapped_query, zero), jnp.where(low, zero, query), swapped_values, values
    )
    o_ref[...] = jnp.where(low, even_rows, odd_rows).astype(o_ref.dtype)


def attention(packed, even_bias, odd_bias, block_rows=128, interpret=False):
    rows, width = packed.shape
    lanes = width // 3
    swapped = jnp.concatenate(
        [jnp.roll(packed[:, :lanes], HEAD, axis=1), jnp.roll(packed[:, 2 * lanes :], HEAD, axis=1)],
        axis=1,
    )
    return pl.pallas_call(
        attention_kernel,
        grid=(rows // block_rows,),
        in_specs=[
            pl.BlockSpec((rows, width), lambda i: (0, 0)),
            pl.BlockSpec((rows, 2 * lanes), lambda i: (0, 0)),
            pl.BlockSpec((1, rows), lambda i: (0, 0)),
            pl.BlockSpec((1, rows), lambda i: (0, 0)),
        ],
        out_specs=pl.BlockSpec((block_rows, lanes), lambda i: (i, 0)),
        out_shape=jax.ShapeDtypeStruct((rows, lanes), jnp.bfloat16),
        compiler_params=pltpu.CompilerParams(vmem_limit_bytes=48 * 1024 * 1024),
        interpret=interpret,
    )(packed, swapped, even_bias, odd_bias)


def modulate(hidden, row_mean, spread, shift_part, gain_part):
    return (
        (hidden - row_mean) / jnp.sqrt(spread + ln_epsilon) * (1.0 + gain_part) + shift_part
    ).astype(jnp.bfloat16)


def body(projected, lengths, text_len, out_weight, modulation, proj_weight, latent, timestep):
    seq_count = lax.axis_size("seq")
    item_count, capacity = (projected.shape[1], projected.shape[2])
    attn_width = projected.shape[3] // 3
    group_width = attn_width // seq_count
    slot_count = capacity * seq_count
    half_cap = capacity // 2
    heads_here = group_width // HEAD
    outgoing = projected[0, 0].reshape(half_cap, 2, 3, seq_count, heads_here, HEAD)
    outgoing = outgoing.transpose(4, 3, 0, 2, 1, 5).reshape(
        heads_here, seq_count, half_cap, 3 * 2 * HEAD
    )
    key_slots, unused_video = slot_masks(
        lengths, text_len, jnp.arange(slot_count, dtype=jnp.int32), capacity
    )
    bias = jnp.where(key_slots, 0.0, -jnp.inf).astype(jnp.float32)
    bias = bias.reshape(seq_count * half_cap, 2)
    even_bias = bias[:, 0].reshape(1, -1)
    odd_bias = bias[:, 1].reshape(1, -1)
    pieces = []
    for head in range(heads_here):
        arrived = lax.all_to_all(outgoing[head], "seq", split_axis=0, concat_axis=0, tiled=True)
        attended = attention(arrived.reshape(seq_count * half_cap, 3 * 2 * HEAD), even_bias, odd_bias)
        pieces.append(
            lax.all_to_all(
                attended.reshape(seq_count, half_cap, 2 * HEAD),
                "seq",
                split_axis=0,
                concat_axis=0,
                tiled=True,
            )
        )
    returned = jnp.stack(pieces).reshape(heads_here, seq_count, half_cap, 2, HEAD)
    returned = returned.transpose(1, 2, 3, 0, 4).reshape(seq_count, capacity, group_width)
    cfg_index = lax.axis_index("cfg")
    weight_half = lax.all_gather(out_weight, "seq", axis=0, tiled=True)
    partner_rows = partner_2(returned, "cfg", 0)
    own_first = cfg_index == 0
    both = jnp.stack(
        [jnp.where(own_first, returned, partner_rows), jnp.where(own_first, partner_rows, returned)]
    )
    hidden = jnp.einsum(
        "agsj,gjc->asc",
        both,
        weight_half.reshape(seq_count, group_width, out_weight.shape[1]),
        preferred_element_type=jnp.float32,
    )
    half_width = out_weight.shape[1]
    column_start = cfg_index * half_width
    sums = jnp.stack([jnp.sum(hidden, axis=2), jnp.sum(hidden * hidden, axis=2)])
    sums = sums + partner_2(sums, "cfg", 0)
    row_mean = (sums[0] / D)[:, :, None]
    spread = (sums[1] / D)[:, :, None] - row_mean * row_mean
    shift_part = lax.dynamic_slice_in_dim(modulation[0, 0], column_start, half_width, 0)
    gain_part = lax.dynamic_slice_in_dim(modulation[0, 1], column_start, half_width, 0)
    normed = modulate(hidden, row_mean, spread, shift_part, gain_part)
    proj_half = lax.dynamic_slice_in_dim(proj_weight, column_start, half_width, 0)
    velocity = jnp.dot(
        normed.reshape(2 * capacity, half_width), proj_half, preferred_element_type=jnp.float32
    ).reshape(2, capacity, 2, OUT_CH // 2)
    own_half = jnp.where(own_first, velocity[:, :, 0], velocity[:, :, 1])
    other_half = jnp.where(own_first, velocity[:, :, 1], velocity[:, :, 0])
    velocity = own_half + partner_2(other_half, "cfg", 0)
    conditional = velocity[0][None]
    unconditional = velocity[1][None]
    own_slots = lax.axis_index("seq") * capacity + jnp.arange(capacity, dtype=jnp.int32)
    unused_keys, video_slots = slot_masks(lengths, text_len, own_slots, capacity)
    video_mask = video_slots[:, :, None]
    guided = jnp.where(video_mask, unconditional + guide_scale * (conditional - unconditional), 0.0)
    alpha_now, alpha_prev = plan(timestep)
    clean_part = jnp.sqrt(alpha_now) * latent - jnp.sqrt(1.0 - alpha_now) * guided
    noise_part = jnp.sqrt(1.0 - alpha_now) * latent + jnp.sqrt(alpha_now) * guided
    previous = jnp.where(
        video_mask, jnp.sqrt(alpha_prev) * clean_part + jnp.sqrt(1.0 - alpha_prev) * noise_part, 0.0
    )
    return (guided, previous)


def solution(mesh):
    placed = (
        P("cfg", "req", "seq", None),
        P("req", None),
        P("req"),
        P("seq", "cfg"),
        P("req", None, None),
        P(),
        P("req", "seq", "cfg"),
        P("req"),
    )
    return jax.shard_map(
        body,
        mesh=mesh,
        in_specs=placed,
        out_specs=(P("req", "seq", "cfg"), P("req", "seq", "cfg")),
        check_vma=False,
    )
```

```python
import math

import jax
import jax.numpy as jnp
from jax import lax
from jax.sharding import PartitionSpec as P
from jax.experimental import pallas as pl
from jax.experimental.pallas import tpu as pltpu

D = 3072
HEAD = 64
OUT_CH = 64
TEXT = 226


guide_scale = 6.0
ln_epsilon = 1e-05
step_gap = 20


def partner_2(array, axis, bit):
    return lax.ppermute(array, axis, [(i, i ^ 1 << bit) for i in range(lax.axis_size(axis))])


def slot_masks(lengths, text_len, slot_ids, capacity):
    piece_ids = slot_ids // capacity
    local_ids = slot_ids % capacity
    seq_ids = jnp.arange(lengths.shape[1], dtype=jnp.int32)
    select = (piece_ids[None, :] == seq_ids[:, None]).astype(jnp.int32)
    offsets = jnp.cumsum(lengths, axis=1) - lengths
    piece_len = jnp.sum(lengths[:, :, None] * select[None], axis=1)
    start_pos = jnp.sum(offsets[:, :, None] * select[None], axis=1)
    position = start_pos + local_ids[None, :]
    live_slots = local_ids[None, :] < piece_len
    key_slots = live_slots & ((position >= TEXT) | (position < text_len[:, None]))
    video_slots = live_slots & (position >= TEXT)
    return (key_slots, video_slots)


def plan(timestep):
    indices = jnp.arange(1000, dtype=jnp.int32)
    counter = jnp.arange(1000, dtype=jnp.float32)
    root_beta = math.sqrt(0.00085) + (math.sqrt(0.012) - math.sqrt(0.00085)) * counter / 999.0
    log_keep = jnp.log1p(-root_beta * root_beta)
    current = timestep[0]
    earlier = jnp.maximum(current - step_gap, 0)
    alpha_now = jnp.exp(jnp.sum(jnp.where(indices <= current, log_keep, 0.0)))
    alpha_prev = jnp.exp(jnp.sum(jnp.where(indices <= earlier, log_keep, 0.0)))
    return (alpha_now, alpha_prev)


def attention_kernel(x_ref, bias_ref, o_ref):
    block = o_ref.shape[0]
    start = pl.multiple_of(pl.program_id(0) * block, block)
    query = x_ref[pl.ds(start, block), 0:128]
    keyset = x_ref[:, 128:256]
    values = x_ref[:, 256:384]
    bias = bias_ref[...]
    lane = lax.broadcasted_iota(jnp.int32, query.shape, 1)
    results = []
    for head in range(2):
        own = (lane >= HEAD) if head else (lane < HEAD)
        masked = jnp.where(own, query, jnp.zeros_like(query))
        scores = lax.dot_general(
            masked, keyset, (((1,), (1,)), ((), ())), preferred_element_type=jnp.float32
        )
        scores = scores * (1.0 / math.sqrt(HEAD)) + bias
        row_top = jnp.max(scores, axis=1, keepdims=True)
        weights = jnp.exp(scores - row_top)
        total = jnp.sum(weights, axis=1, keepdims=True)
        probs = (weights * (1.0 / total)).astype(jnp.bfloat16)
        results.append(jnp.dot(probs, values, preferred_element_type=jnp.float32))
    o_ref[...] = jnp.where(lane < HEAD, results[0], results[1]).astype(o_ref.dtype)


def attention(grouped, bias, block_rows=256):
    slot_count, width = grouped.shape
    return pl.pallas_call(
        attention_kernel,
        grid=(slot_count // block_rows,),
        in_specs=[
            pl.BlockSpec((slot_count, width), lambda i: (0, 0)),
            pl.BlockSpec((1, slot_count), lambda i: (0, 0)),
        ],
        out_specs=pl.BlockSpec((block_rows, width // 3), lambda i: (i, 0)),
        out_shape=jax.ShapeDtypeStruct((slot_count, width // 3), jnp.bfloat16),
        compiler_params=pltpu.CompilerParams(vmem_limit_bytes=48 * 1024 * 1024),
    )(grouped, bias)


def modulate(hidden, row_mean, spread, shift_part, gain_part):
    return (
        (hidden - row_mean) / jnp.sqrt(spread + ln_epsilon) * (1.0 + gain_part) + shift_part
    ).astype(jnp.bfloat16)


def body(projected, lengths, text_len, out_weight, modulation, proj_weight, latent, timestep):
    seq_count = lax.axis_size("seq")
    item_count, capacity = (projected.shape[1], projected.shape[2])
    attn_width = projected.shape[3] // 3
    group_width = attn_width // seq_count
    slot_count = capacity * seq_count
    outgoing = projected[0, 0].reshape(capacity, 3, seq_count, group_width)
    outgoing = outgoing.transpose(2, 0, 1, 3)
    arrived = lax.all_to_all(outgoing, "seq", split_axis=0, concat_axis=0, tiled=True)
    grouped = arrived.reshape(slot_count, 3 * group_width)
    out_weight = out_weight + arrived[0, 0, 0, 0] * jnp.zeros((), out_weight.dtype)
    key_slots, unused_video = slot_masks(
        lengths, text_len, jnp.arange(slot_count, dtype=jnp.int32), capacity
    )
    bias = jnp.where(key_slots, 0.0, -jnp.inf).astype(jnp.float32)
    attended = attention(grouped, bias)
    returned = lax.all_to_all(
        attended.reshape(seq_count, capacity, group_width),
        "seq",
        split_axis=0,
        concat_axis=0,
        tiled=True,
    )
    cfg_index = lax.axis_index("cfg")
    weight_half = lax.all_gather(out_weight, "seq", axis=0, tiled=True)
    partner_rows = partner_2(returned, "cfg", 0)
    own_first = cfg_index == 0
    both = jnp.stack(
        [jnp.where(own_first, returned, partner_rows), jnp.where(own_first, partner_rows, returned)]
    )
    hidden = jnp.einsum(
        "agsj,gjc->asc",
        both,
        weight_half.reshape(seq_count, group_width, out_weight.shape[1]),
        preferred_element_type=jnp.float32,
    )
    half_width = out_weight.shape[1]
    column_start = cfg_index * half_width
    sums = jnp.stack([jnp.sum(hidden, axis=2), jnp.sum(hidden * hidden, axis=2)])
    sums = sums + partner_2(sums, "cfg", 0)
    row_mean = (sums[0] / D)[:, :, None]
    spread = (sums[1] / D)[:, :, None] - row_mean * row_mean
    shift_part = lax.dynamic_slice_in_dim(modulation[0, 0], column_start, half_width, 0)
    gain_part = lax.dynamic_slice_in_dim(modulation[0, 1], column_start, half_width, 0)
    normed = modulate(hidden, row_mean, spread, shift_part, gain_part)
    proj_half = lax.dynamic_slice_in_dim(proj_weight, column_start, half_width, 0)
    velocity = jnp.dot(
        normed.reshape(2 * capacity, half_width), proj_half, preferred_element_type=jnp.float32
    ).reshape(2, capacity, 2, OUT_CH // 2)
    own_half = jnp.where(own_first, velocity[:, :, 0], velocity[:, :, 1])
    other_half = jnp.where(own_first, velocity[:, :, 1], velocity[:, :, 0])
    velocity = own_half + partner_2(other_half, "cfg", 0)
    conditional = velocity[0][None]
    unconditional = velocity[1][None]
    own_slots = lax.axis_index("seq") * capacity + jnp.arange(capacity, dtype=jnp.int32)
    unused_keys, video_slots = slot_masks(lengths, text_len, own_slots, capacity)
    video_mask = video_slots[:, :, None]
    guided = jnp.where(video_mask, unconditional + guide_scale * (conditional - unconditional), 0.0)
    alpha_now, alpha_prev = plan(timestep)
    clean_part = jnp.sqrt(alpha_now) * latent - jnp.sqrt(1.0 - alpha_now) * guided
    noise_part = jnp.sqrt(1.0 - alpha_now) * latent + jnp.sqrt(alpha_now) * guided
    previous = jnp.where(
        video_mask, jnp.sqrt(alpha_prev) * clean_part + jnp.sqrt(1.0 - alpha_prev) * noise_part, 0.0
    )
    return (guided, previous)


def solution(mesh):
    placed = (
        P("cfg", "req", "seq", None),
        P("req", None),
        P("req"),
        P("seq", "cfg"),
        P("req", None, None),
        P(),
        P("req", "seq", "cfg"),
        P("req"),
    )
    return jax.shard_map(
        body,
        mesh=mesh,
        in_specs=placed,
        out_specs=(P("req", "seq", "cfg"), P("req", "seq", "cfg")),
        check_vma=False,
    )
```

```python
import functools
import math

import jax
import jax.numpy as jnp
from jax import lax
from jax.sharding import PartitionSpec as P
from jax.experimental import pallas as pl
from jax.experimental.pallas import tpu as pltpu

D = 3072
HEAD = 64
OUT_CH = 64
TEXT = 226


guide_scale = 6.0
ln_epsilon = 1e-05
step_gap = 20


def partner_2(array, axis, bit):
    return lax.ppermute(array, axis, [(i, i ^ 1 << bit) for i in range(lax.axis_size(axis))])


def slot_masks(lengths, text_len, slot_ids, capacity):
    piece_ids = slot_ids // capacity
    local_ids = slot_ids % capacity
    seq_ids = jnp.arange(lengths.shape[1], dtype=jnp.int32)
    select = (piece_ids[None, :] == seq_ids[:, None]).astype(jnp.int32)
    offsets = jnp.cumsum(lengths, axis=1) - lengths
    piece_len = jnp.sum(lengths[:, :, None] * select[None], axis=1)
    start_pos = jnp.sum(offsets[:, :, None] * select[None], axis=1)
    position = start_pos + local_ids[None, :]
    live_slots = local_ids[None, :] < piece_len
    key_slots = live_slots & ((position >= TEXT) | (position < text_len[:, None]))
    video_slots = live_slots & (position >= TEXT)
    return (key_slots, video_slots)


def plan(timestep):
    indices = jnp.arange(1000, dtype=jnp.int32)
    counter = jnp.arange(1000, dtype=jnp.float32)
    root_beta = math.sqrt(0.00085) + (math.sqrt(0.012) - math.sqrt(0.00085)) * counter / 999.0
    log_keep = jnp.log1p(-root_beta * root_beta)
    current = timestep[0]
    earlier = jnp.maximum(current - step_gap, 0)
    alpha_now = jnp.exp(jnp.sum(jnp.where(indices <= current, log_keep, 0.0)))
    alpha_prev = jnp.exp(jnp.sum(jnp.where(indices <= earlier, log_keep, 0.0)))
    return (alpha_now, alpha_prev)


def attention_kernel(q_ref, kv_ref, bias_ref, *rest, second):
    o_ref = rest[-1]
    block = o_ref.shape[0]
    start = pl.multiple_of(pl.program_id(0) * block, block)
    query = q_ref[pl.ds(start, block), 0:128]
    pair = kv_ref[:, kv_ref.shape[1] - 128 :]
    low = lax.broadcasted_iota(jnp.int32, query.shape, 1) < HEAD
    masked = jnp.where(low, jnp.zeros_like(query), query) if second else jnp.where(
        low, query, jnp.zeros_like(query)
    )
    scores = lax.dot_general(
        masked, pair, (((1,), (1,)), ((), ())), preferred_element_type=jnp.float32
    )
    scores = scores * (1.0 / math.sqrt(HEAD)) + bias_ref[...]
    row_top = jnp.max(scores, axis=1, keepdims=True)
    weights = jnp.exp(scores - row_top)
    total = jnp.sum(weights, axis=1, keepdims=True)
    probs = (weights * (1.0 / total)).astype(jnp.bfloat16)
    result = jnp.dot(probs, pair, preferred_element_type=jnp.float32)
    if second:
        result = jnp.where(low, result, rest[0][...].astype(jnp.float32))
    o_ref[...] = result.astype(o_ref.dtype)


def attention(first_part, second_part, bias, earlier=None, block_rows=256):
    slot_count = first_part.shape[0]
    second = earlier is not None
    operands = [first_part, second_part if second else first_part, bias]
    in_specs = [
        pl.BlockSpec(first_part.shape, lambda i: (0, 0)),
        pl.BlockSpec(operands[1].shape, lambda i: (0, 0)),
        pl.BlockSpec((1, slot_count), lambda i: (0, 0)),
    ]
    if second:
        operands.append(earlier)
        in_specs.append(pl.BlockSpec((block_rows, 128), lambda i: (i, 0)))
    return pl.pallas_call(
        functools.partial(attention_kernel, second=second),
        grid=(slot_count // block_rows,),
        in_specs=in_specs,
        out_specs=pl.BlockSpec((block_rows, 128), lambda i: (i, 0)),
        out_shape=jax.ShapeDtypeStruct((slot_count, 128), jnp.bfloat16),
        compiler_params=pltpu.CompilerParams(vmem_limit_bytes=48 * 1024 * 1024),
    )(*operands)


def modulate(hidden, row_mean, spread, shift_part, gain_part):
    return (
        (hidden - row_mean) / jnp.sqrt(spread + ln_epsilon) * (1.0 + gain_part) + shift_part
    ).astype(jnp.bfloat16)


def body(projected, lengths, text_len, out_weight, modulation, proj_weight, latent, timestep):
    seq_count = lax.axis_size("seq")
    item_count, capacity = (projected.shape[1], projected.shape[2])
    attn_width = projected.shape[3] // 3
    group_width = attn_width // seq_count
    slot_count = capacity * seq_count
    split = projected[0, 0].reshape(capacity, 3, seq_count, 2, HEAD)
    first_send = jnp.concatenate(
        [split[:, 0].reshape(capacity, seq_count, 2 * HEAD), split[:, 1, :, 0], split[:, 2, :, 0]],
        axis=-1,
    ).transpose(1, 0, 2)
    second_send = jnp.concatenate([split[:, 2, :, 1], split[:, 1, :, 1]], axis=-1).transpose(1, 0, 2)
    arrived = lax.all_to_all(first_send, "seq", split_axis=0, concat_axis=0, tiled=True)
    later = lax.all_to_all(second_send, "seq", split_axis=0, concat_axis=0, tiled=True)
    out_weight = out_weight + arrived[0, 0, 0] * jnp.zeros((), out_weight.dtype)
    out_weight = jnp.roll(out_weight, HEAD, axis=0)
    key_slots, unused_video = slot_masks(
        lengths, text_len, jnp.arange(slot_count, dtype=jnp.int32), capacity
    )
    bias = jnp.where(key_slots, 0.0, -jnp.inf).astype(jnp.float32)
    arrived = arrived.reshape(slot_count, 4 * HEAD)
    attended = attention(arrived, arrived, bias)
    attended = attention(arrived, later.reshape(slot_count, 2 * HEAD), bias, attended)
    returned = lax.all_to_all(
        attended.reshape(seq_count, capacity, group_width),
        "seq",
        split_axis=0,
        concat_axis=0,
        tiled=True,
    )
    cfg_index = lax.axis_index("cfg")
    weight_half = lax.all_gather(out_weight, "seq", axis=0, tiled=True)
    partner_rows = partner_2(returned, "cfg", 0)
    own_first = cfg_index == 0
    both = jnp.stack(
        [jnp.where(own_first, returned, partner_rows), jnp.where(own_first, partner_rows, returned)]
    )
    hidden = jnp.einsum(
        "agsj,gjc->asc",
        both,
        weight_half.reshape(seq_count, group_width, out_weight.shape[1]),
        preferred_element_type=jnp.float32,
    )
    half_width = out_weight.shape[1]
    column_start = cfg_index * half_width
    sums = jnp.stack([jnp.sum(hidden, axis=2), jnp.sum(hidden * hidden, axis=2)])
    sums = sums + partner_2(sums, "cfg", 0)
    row_mean = (sums[0] / D)[:, :, None]
    spread = (sums[1] / D)[:, :, None] - row_mean * row_mean
    shift_part = lax.dynamic_slice_in_dim(modulation[0, 0], column_start, half_width, 0)
    gain_part = lax.dynamic_slice_in_dim(modulation[0, 1], column_start, half_width, 0)
    normed = modulate(hidden, row_mean, spread, shift_part, gain_part)
    proj_half = lax.dynamic_slice_in_dim(proj_weight, column_start, half_width, 0)
    velocity = jnp.dot(
        normed.reshape(2 * capacity, half_width), proj_half, preferred_element_type=jnp.float32
    ).reshape(2, capacity, 2, OUT_CH // 2)
    own_half = jnp.where(own_first, velocity[:, :, 0], velocity[:, :, 1])
    other_half = jnp.where(own_first, velocity[:, :, 1], velocity[:, :, 0])
    velocity = own_half + partner_2(other_half, "cfg", 0)
    conditional = velocity[0][None]
    unconditional = velocity[1][None]
    own_slots = lax.axis_index("seq") * capacity + jnp.arange(capacity, dtype=jnp.int32)
    unused_keys, video_slots = slot_masks(lengths, text_len, own_slots, capacity)
    video_mask = video_slots[:, :, None]
    guided = jnp.where(video_mask, unconditional + guide_scale * (conditional - unconditional), 0.0)
    alpha_now, alpha_prev = plan(timestep)
    clean_part = jnp.sqrt(alpha_now) * latent - jnp.sqrt(1.0 - alpha_now) * guided
    noise_part = jnp.sqrt(1.0 - alpha_now) * latent + jnp.sqrt(alpha_now) * guided
    previous = jnp.where(
        video_mask, jnp.sqrt(alpha_prev) * clean_part + jnp.sqrt(1.0 - alpha_prev) * noise_part, 0.0
    )
    return (guided, previous)


def solution(mesh):
    placed = (
        P("cfg", "req", "seq", None),
        P("req", None),
        P("req"),
        P("seq", "cfg"),
        P("req", None, None),
        P(),
        P("req", "seq", "cfg"),
        P("req"),
    )
    return jax.shard_map(
        body,
        mesh=mesh,
        in_specs=placed,
        out_specs=(P("req", "seq", "cfg"), P("req", "seq", "cfg")),
        check_vma=False,
    )
```

```python
import functools
import math

import jax
import jax.numpy as jnp
from jax import lax
from jax.sharding import PartitionSpec as P
from jax.experimental import pallas as pl
from jax.experimental.pallas import tpu as pltpu

D = 3072
HEAD = 64
OUT_CH = 64
TEXT = 226


guide_scale = 6.0
ln_epsilon = 1e-05
step_gap = 20


def partner_2(array, axis, bit):
    return lax.ppermute(array, axis, [(i, i ^ 1 << bit) for i in range(lax.axis_size(axis))])


def slot_masks(lengths, text_len, slot_ids, capacity):
    piece_ids = slot_ids // capacity
    local_ids = slot_ids % capacity
    seq_ids = jnp.arange(lengths.shape[1], dtype=jnp.int32)
    select = (piece_ids[None, :] == seq_ids[:, None]).astype(jnp.int32)
    offsets = jnp.cumsum(lengths, axis=1) - lengths
    piece_len = jnp.sum(lengths[:, :, None] * select[None], axis=1)
    start_pos = jnp.sum(offsets[:, :, None] * select[None], axis=1)
    position = start_pos + local_ids[None, :]
    live_slots = local_ids[None, :] < piece_len
    key_slots = live_slots & ((position >= TEXT) | (position < text_len[:, None]))
    video_slots = live_slots & (position >= TEXT)
    return (key_slots, video_slots)


def plan(timestep):
    indices = jnp.arange(1000, dtype=jnp.int32)
    counter = jnp.arange(1000, dtype=jnp.float32)
    root_beta = math.sqrt(0.00085) + (math.sqrt(0.012) - math.sqrt(0.00085)) * counter / 999.0
    log_keep = jnp.log1p(-root_beta * root_beta)
    current = timestep[0]
    earlier = jnp.maximum(current - step_gap, 0)
    alpha_now = jnp.exp(jnp.sum(jnp.where(indices <= current, log_keep, 0.0)))
    alpha_prev = jnp.exp(jnp.sum(jnp.where(indices <= earlier, log_keep, 0.0)))
    return (alpha_now, alpha_prev)


def attention_kernel(x_ref, bias_ref, o_ref, *, part):
    step_pieces, rows = o_ref.shape[0], o_ref.shape[1]
    capacity = rows * 2
    first_piece = pl.program_id(0) * step_pieces
    query = jnp.concatenate(
        [
            x_ref[pl.ds(pl.multiple_of((first_piece + j) * capacity + part * rows, 16), rows), 0:128]
            for j in range(step_pieces)
        ],
        axis=0,
    )
    keyset = x_ref[:, 128:256]
    values = x_ref[:, 256:384]
    bias = bias_ref[...]
    lane = lax.broadcasted_iota(jnp.int32, query.shape, 1)
    results = []
    for head in range(2):
        own = (lane >= HEAD) if head else (lane < HEAD)
        masked = jnp.where(own, query, jnp.zeros_like(query))
        scores = lax.dot_general(
            masked, keyset, (((1,), (1,)), ((), ())), preferred_element_type=jnp.float32
        )
        scores = scores * (1.0 / math.sqrt(HEAD)) + bias
        row_top = jnp.max(scores, axis=1, keepdims=True)
        weights = jnp.exp(scores - row_top)
        total = jnp.sum(weights, axis=1, keepdims=True)
        probs = (weights * (1.0 / total)).astype(jnp.bfloat16)
        results.append(jnp.dot(probs, values, preferred_element_type=jnp.float32))
    out = jnp.where(lane < HEAD, results[0], results[1]).astype(o_ref.dtype)
    o_ref[...] = out.reshape(o_ref.shape)


def attention(pieces, bias, part, parts=2, pieces_per_step=2):
    piece_count, capacity, width = pieces.shape
    rows = capacity // parts
    flat = pieces.reshape(piece_count * capacity, width)
    return pl.pallas_call(
        functools.partial(attention_kernel, part=part),
        grid=(piece_count // pieces_per_step,),
        in_specs=[
            pl.BlockSpec(flat.shape, lambda i: (0, 0)),
            pl.BlockSpec((1, piece_count * capacity), lambda i: (0, 0)),
        ],
        out_specs=pl.BlockSpec((pieces_per_step, rows, width // 3), lambda i: (i, 0, 0)),
        out_shape=jax.ShapeDtypeStruct((piece_count, rows, width // 3), jnp.bfloat16),
        compiler_params=pltpu.CompilerParams(vmem_limit_bytes=48 * 1024 * 1024),
    )(flat, bias)


def modulate(hidden, row_mean, spread, shift_part, gain_part):
    return (
        (hidden - row_mean) / jnp.sqrt(spread + ln_epsilon) * (1.0 + gain_part) + shift_part
    ).astype(jnp.bfloat16)


def body(projected, lengths, text_len, out_weight, modulation, proj_weight, latent, timestep):
    seq_count = lax.axis_size("seq")
    item_count, capacity = (projected.shape[1], projected.shape[2])
    attn_width = projected.shape[3] // 3
    group_width = attn_width // seq_count
    slot_count = capacity * seq_count
    outgoing = projected[0, 0].reshape(capacity, 3, seq_count, group_width)
    outgoing = outgoing.transpose(2, 0, 1, 3)
    arrived = lax.all_to_all(outgoing, "seq", split_axis=0, concat_axis=0, tiled=True)
    grouped = arrived.reshape(slot_count, 3 * group_width)
    out_weight = out_weight + arrived[0, 0, 0, 0] * jnp.zeros((), out_weight.dtype)
    key_slots, unused_video = slot_masks(
        lengths, text_len, jnp.arange(slot_count, dtype=jnp.int32), capacity
    )
    bias = jnp.where(key_slots, 0.0, -jnp.inf).astype(jnp.float32)
    pieces = grouped.reshape(seq_count, capacity, 3 * group_width)
    halves = []
    for part in range(2):
        attended = attention(pieces, bias, part)
        halves.append(
            lax.all_to_all(attended, "seq", split_axis=0, concat_axis=0, tiled=True)
        )
    returned = jnp.concatenate(halves, axis=1)
    cfg_index = lax.axis_index("cfg")
    weight_half = lax.all_gather(out_weight, "seq", axis=0, tiled=True)
    partner_rows = partner_2(returned, "cfg", 0)
    own_first = cfg_index == 0
    both = jnp.stack(
        [jnp.where(own_first, returned, partner_rows), jnp.where(own_first, partner_rows, returned)]
    )
    hidden = jnp.einsum(
        "agsj,gjc->asc",
        both,
        weight_half.reshape(seq_count, group_width, out_weight.shape[1]),
        preferred_element_type=jnp.float32,
    )
    half_width = out_weight.shape[1]
    column_start = cfg_index * half_width
    sums = jnp.stack([jnp.sum(hidden, axis=2), jnp.sum(hidden * hidden, axis=2)])
    sums = sums + partner_2(sums, "cfg", 0)
    row_mean = (sums[0] / D)[:, :, None]
    spread = (sums[1] / D)[:, :, None] - row_mean * row_mean
    shift_part = lax.dynamic_slice_in_dim(modulation[0, 0], column_start, half_width, 0)
    gain_part = lax.dynamic_slice_in_dim(modulation[0, 1], column_start, half_width, 0)
    normed = modulate(hidden, row_mean, spread, shift_part, gain_part)
    proj_half = lax.dynamic_slice_in_dim(proj_weight, column_start, half_width, 0)
    velocity = jnp.dot(
        normed.reshape(2 * capacity, half_width), proj_half, preferred_element_type=jnp.float32
    ).reshape(2, capacity, 2, OUT_CH // 2)
    own_half = jnp.where(own_first, velocity[:, :, 0], velocity[:, :, 1])
    other_half = jnp.where(own_first, velocity[:, :, 1], velocity[:, :, 0])
    velocity = own_half + partner_2(other_half, "cfg", 0)
    conditional = velocity[0][None]
    unconditional = velocity[1][None]
    own_slots = lax.axis_index("seq") * capacity + jnp.arange(capacity, dtype=jnp.int32)
    unused_keys, video_slots = slot_masks(lengths, text_len, own_slots, capacity)
    video_mask = video_slots[:, :, None]
    guided = jnp.where(video_mask, unconditional + guide_scale * (conditional - unconditional), 0.0)
    alpha_now, alpha_prev = plan(timestep)
    clean_part = jnp.sqrt(alpha_now) * latent - jnp.sqrt(1.0 - alpha_now) * guided
    noise_part = jnp.sqrt(1.0 - alpha_now) * latent + jnp.sqrt(alpha_now) * guided
    previous = jnp.where(
        video_mask, jnp.sqrt(alpha_prev) * clean_part + jnp.sqrt(1.0 - alpha_prev) * noise_part, 0.0
    )
    return (guided, previous)


def solution(mesh):
    placed = (
        P("cfg", "req", "seq", None),
        P("req", None),
        P("req"),
        P("seq", "cfg"),
        P("req", None, None),
        P(),
        P("req", "seq", "cfg"),
        P("req"),
    )
    return jax.shard_map(
        body,
        mesh=mesh,
        in_specs=placed,
        out_specs=(P("req", "seq", "cfg"), P("req", "seq", "cfg")),
        check_vma=False,
    )
```

```python
import functools
import math

import jax
import jax.numpy as jnp
from jax import lax
from jax.sharding import PartitionSpec as P
from jax.experimental import pallas as pl
from jax.experimental.pallas import tpu as pltpu

D = 3072
HEAD = 64
OUT_CH = 64
TEXT = 226


guide_scale = 6.0
ln_epsilon = 1e-05
step_gap = 20


def partner_2(array, axis, bit):
    return lax.ppermute(array, axis, [(i, i ^ 1 << bit) for i in range(lax.axis_size(axis))])


def slot_masks(lengths, text_len, slot_ids, capacity):
    piece_ids = slot_ids // capacity
    local_ids = slot_ids % capacity
    seq_ids = jnp.arange(lengths.shape[1], dtype=jnp.int32)
    select = (piece_ids[None, :] == seq_ids[:, None]).astype(jnp.int32)
    offsets = jnp.cumsum(lengths, axis=1) - lengths
    piece_len = jnp.sum(lengths[:, :, None] * select[None], axis=1)
    start_pos = jnp.sum(offsets[:, :, None] * select[None], axis=1)
    position = start_pos + local_ids[None, :]
    live_slots = local_ids[None, :] < piece_len
    key_slots = live_slots & ((position >= TEXT) | (position < text_len[:, None]))
    video_slots = live_slots & (position >= TEXT)
    return (key_slots, video_slots)


def plan(timestep):
    indices = jnp.arange(1000, dtype=jnp.int32)
    counter = jnp.arange(1000, dtype=jnp.float32)
    root_beta = math.sqrt(0.00085) + (math.sqrt(0.012) - math.sqrt(0.00085)) * counter / 999.0
    log_keep = jnp.log1p(-root_beta * root_beta)
    current = timestep[0]
    earlier = jnp.maximum(current - step_gap, 0)
    alpha_now = jnp.exp(jnp.sum(jnp.where(indices <= current, log_keep, 0.0)))
    alpha_prev = jnp.exp(jnp.sum(jnp.where(indices <= earlier, log_keep, 0.0)))
    return (alpha_now, alpha_prev)


def attention_kernel(x_ref, bias_ref, o_ref, *, row_start, capacity):
    step_pieces, rows = o_ref.shape[0], o_ref.shape[1]
    first_piece = pl.program_id(0) * step_pieces
    query = jnp.concatenate(
        [
            x_ref[pl.ds(pl.multiple_of((first_piece + j) * capacity + row_start, 16), rows), 0:128]
            for j in range(step_pieces)
        ],
        axis=0,
    )
    keyset = x_ref[:, 128:256]
    values = x_ref[:, 256:384]
    bias = bias_ref[...]
    lane = lax.broadcasted_iota(jnp.int32, query.shape, 1)
    results = []
    for head in range(2):
        own = (lane >= HEAD) if head else (lane < HEAD)
        masked = jnp.where(own, query, jnp.zeros_like(query))
        scores = lax.dot_general(
            masked, keyset, (((1,), (1,)), ((), ())), preferred_element_type=jnp.float32
        )
        scores = scores * (1.0 / math.sqrt(HEAD)) + bias
        row_top = jnp.max(scores, axis=1, keepdims=True)
        weights = jnp.exp(scores - row_top)
        total = jnp.sum(weights, axis=1, keepdims=True)
        probs = (weights * (1.0 / total)).astype(jnp.bfloat16)
        results.append(jnp.dot(probs, values, preferred_element_type=jnp.float32))
    out = jnp.where(lane < HEAD, results[0], results[1]).astype(o_ref.dtype)
    o_ref[...] = out.reshape(o_ref.shape)


def attention(pieces, bias, row_start, rows, pieces_per_step):
    piece_count, capacity, width = pieces.shape
    flat = pieces.reshape(piece_count * capacity, width)
    return pl.pallas_call(
        functools.partial(attention_kernel, row_start=row_start, capacity=capacity),
        grid=(piece_count // pieces_per_step,),
        in_specs=[
            pl.BlockSpec(flat.shape, lambda i: (0, 0)),
            pl.BlockSpec((1, piece_count * capacity), lambda i: (0, 0)),
        ],
        out_specs=pl.BlockSpec((pieces_per_step, rows, width // 3), lambda i: (i, 0, 0)),
        out_shape=jax.ShapeDtypeStruct((piece_count, rows, width // 3), jnp.bfloat16),
        compiler_params=pltpu.CompilerParams(vmem_limit_bytes=48 * 1024 * 1024),
    )(flat, bias)


def modulate(hidden, row_mean, spread, shift_part, gain_part):
    return (
        (hidden - row_mean) / jnp.sqrt(spread + ln_epsilon) * (1.0 + gain_part) + shift_part
    ).astype(jnp.bfloat16)


def body(projected, lengths, text_len, out_weight, modulation, proj_weight, latent, timestep):
    seq_count = lax.axis_size("seq")
    item_count, capacity = (projected.shape[1], projected.shape[2])
    attn_width = projected.shape[3] // 3
    group_width = attn_width // seq_count
    slot_count = capacity * seq_count
    outgoing = projected[0, 0].reshape(capacity, 3, seq_count, group_width)
    outgoing = outgoing.transpose(2, 0, 1, 3)
    arrived = lax.all_to_all(outgoing, "seq", split_axis=0, concat_axis=0, tiled=True)
    grouped = arrived.reshape(slot_count, 3 * group_width)
    out_weight = out_weight + arrived[0, 0, 0, 0] * jnp.zeros((), out_weight.dtype)
    key_slots, unused_video = slot_masks(
        lengths, text_len, jnp.arange(slot_count, dtype=jnp.int32), capacity
    )
    bias = jnp.where(key_slots, 0.0, -jnp.inf).astype(jnp.float32)
    pieces = grouped.reshape(seq_count, capacity, 3 * group_width)
    halves = []
    for row_start, rows, pieces_per_step in ((0, 160, 2), (160, capacity - 160, 4)):
        attended = attention(pieces, bias, row_start, rows, pieces_per_step)
        halves.append(
            lax.all_to_all(attended, "seq", split_axis=0, concat_axis=0, tiled=True)
        )
    returned = jnp.concatenate(halves, axis=1)
    cfg_index = lax.axis_index("cfg")
    weight_half = lax.all_gather(out_weight, "seq", axis=0, tiled=True)
    partner_rows = partner_2(returned, "cfg", 0)
    own_first = cfg_index == 0
    both = jnp.stack(
        [jnp.where(own_first, returned, partner_rows), jnp.where(own_first, partner_rows, returned)]
    )
    hidden = jnp.einsum(
        "agsj,gjc->asc",
        both,
        weight_half.reshape(seq_count, group_width, out_weight.shape[1]),
        preferred_element_type=jnp.float32,
    )
    half_width = out_weight.shape[1]
    column_start = cfg_index * half_width
    sums = jnp.stack([jnp.sum(hidden, axis=2), jnp.sum(hidden * hidden, axis=2)])
    sums = sums + partner_2(sums, "cfg", 0)
    row_mean = (sums[0] / D)[:, :, None]
    spread = (sums[1] / D)[:, :, None] - row_mean * row_mean
    shift_part = lax.dynamic_slice_in_dim(modulation[0, 0], column_start, half_width, 0)
    gain_part = lax.dynamic_slice_in_dim(modulation[0, 1], column_start, half_width, 0)
    normed = modulate(hidden, row_mean, spread, shift_part, gain_part)
    proj_half = lax.dynamic_slice_in_dim(proj_weight, column_start, half_width, 0)
    velocity = jnp.dot(
        normed.reshape(2 * capacity, half_width), proj_half, preferred_element_type=jnp.float32
    ).reshape(2, capacity, 2, OUT_CH // 2)
    own_half = jnp.where(own_first, velocity[:, :, 0], velocity[:, :, 1])
    other_half = jnp.where(own_first, velocity[:, :, 1], velocity[:, :, 0])
    velocity = own_half + partner_2(other_half, "cfg", 0)
    conditional = velocity[0][None]
    unconditional = velocity[1][None]
    own_slots = lax.axis_index("seq") * capacity + jnp.arange(capacity, dtype=jnp.int32)
    unused_keys, video_slots = slot_masks(lengths, text_len, own_slots, capacity)
    video_mask = video_slots[:, :, None]
    guided = jnp.where(video_mask, unconditional + guide_scale * (conditional - unconditional), 0.0)
    alpha_now, alpha_prev = plan(timestep)
    clean_part = jnp.sqrt(alpha_now) * latent - jnp.sqrt(1.0 - alpha_now) * guided
    noise_part = jnp.sqrt(1.0 - alpha_now) * latent + jnp.sqrt(alpha_now) * guided
    previous = jnp.where(
        video_mask, jnp.sqrt(alpha_prev) * clean_part + jnp.sqrt(1.0 - alpha_prev) * noise_part, 0.0
    )
    return (guided, previous)


def solution(mesh):
    placed = (
        P("cfg", "req", "seq", None),
        P("req", None),
        P("req"),
        P("seq", "cfg"),
        P("req", None, None),
        P(),
        P("req", "seq", "cfg"),
        P("req"),
    )
    return jax.shard_map(
        body,
        mesh=mesh,
        in_specs=placed,
        out_specs=(P("req", "seq", "cfg"), P("req", "seq", "cfg")),
        check_vma=False,
    )
```

```python
import math

import jax
import jax.numpy as jnp
from jax import lax
from jax.sharding import PartitionSpec as P
from jax.experimental import pallas as pl
from jax.experimental.pallas import tpu as pltpu

D = 3072
HEAD = 64
OUT_CH = 64
TEXT = 226


guide_scale = 6.0
ln_epsilon = 1e-05
step_gap = 20


def partner_2(array, axis, bit):
    return lax.ppermute(array, axis, [(i, i ^ 1 << bit) for i in range(lax.axis_size(axis))])


def slot_masks(lengths, text_len, slot_ids, capacity):
    piece_ids = slot_ids // capacity
    local_ids = slot_ids % capacity
    seq_ids = jnp.arange(lengths.shape[1], dtype=jnp.int32)
    select = (piece_ids[None, :] == seq_ids[:, None]).astype(jnp.int32)
    offsets = jnp.cumsum(lengths, axis=1) - lengths
    piece_len = jnp.sum(lengths[:, :, None] * select[None], axis=1)
    start_pos = jnp.sum(offsets[:, :, None] * select[None], axis=1)
    position = start_pos + local_ids[None, :]
    live_slots = local_ids[None, :] < piece_len
    key_slots = live_slots & ((position >= TEXT) | (position < text_len[:, None]))
    video_slots = live_slots & (position >= TEXT)
    return (key_slots, video_slots)


def plan(timestep):
    indices = jnp.arange(1000, dtype=jnp.int32)
    counter = jnp.arange(1000, dtype=jnp.float32)
    root_beta = math.sqrt(0.00085) + (math.sqrt(0.012) - math.sqrt(0.00085)) * counter / 999.0
    log_keep = jnp.log1p(-root_beta * root_beta)
    current = timestep[0]
    earlier = jnp.maximum(current - step_gap, 0)
    alpha_now = jnp.exp(jnp.sum(jnp.where(indices <= current, log_keep, 0.0)))
    alpha_prev = jnp.exp(jnp.sum(jnp.where(indices <= earlier, log_keep, 0.0)))
    return (alpha_now, alpha_prev)


def attention_kernel(q_ref, k_ref, v_ref, bias_ref, o_ref):
    query = q_ref[0, 0]
    slot_count = k_ref.shape[0] * k_ref.shape[2]
    keyset = k_ref[...].reshape(slot_count, k_ref.shape[3])
    values = v_ref[...].reshape(slot_count, v_ref.shape[3])
    bias = bias_ref[...]
    lane = lax.broadcasted_iota(jnp.int32, query.shape, 1)
    results = []
    for head in range(2):
        own = (lane >= HEAD) if head else (lane < HEAD)
        masked = jnp.where(own, query, jnp.zeros_like(query))
        scores = lax.dot_general(
            masked, keyset, (((1,), (1,)), ((), ())), preferred_element_type=jnp.float32
        )
        scores = scores * (1.0 / math.sqrt(HEAD)) + bias
        row_top = jnp.max(scores, axis=1, keepdims=True)
        weights = jnp.exp(scores - row_top)
        total = jnp.sum(weights, axis=1, keepdims=True)
        probs = (weights * (1.0 / total)).astype(jnp.bfloat16)
        results.append(jnp.dot(probs, values, preferred_element_type=jnp.float32))
    o_ref[...] = jnp.where(lane < HEAD, results[0], results[1]).astype(o_ref.dtype)


def attention(blocks, bias):
    piece_count, unused, capacity, width = blocks.shape
    whole = (piece_count, 1, capacity, width)
    return pl.pallas_call(
        attention_kernel,
        grid=(piece_count,),
        in_specs=[
            pl.BlockSpec((1, 1, capacity, width), lambda i: (i, 0, 0, 0)),
            pl.BlockSpec(whole, lambda i: (0, 1, 0, 0)),
            pl.BlockSpec(whole, lambda i: (0, 2, 0, 0)),
            pl.BlockSpec((1, piece_count * capacity), lambda i: (0, 0)),
        ],
        out_specs=pl.BlockSpec((capacity, width), lambda i: (i, 0)),
        out_shape=jax.ShapeDtypeStruct((piece_count * capacity, width), jnp.bfloat16),
        compiler_params=pltpu.CompilerParams(vmem_limit_bytes=48 * 1024 * 1024),
    )(blocks, blocks, blocks, bias)


def modulate(hidden, row_mean, spread, shift_part, gain_part):
    return (
        (hidden - row_mean) / jnp.sqrt(spread + ln_epsilon) * (1.0 + gain_part) + shift_part
    ).astype(jnp.bfloat16)


def body(projected, lengths, text_len, out_weight, modulation, proj_weight, latent, timestep):
    seq_count = lax.axis_size("seq")
    item_count, capacity = (projected.shape[1], projected.shape[2])
    attn_width = projected.shape[3] // 3
    group_width = attn_width // seq_count
    slot_count = capacity * seq_count
    outgoing = projected[0, 0].reshape(capacity, 3, seq_count, group_width)
    outgoing = outgoing.transpose(2, 1, 0, 3)
    arrived = lax.all_to_all(outgoing, "seq", split_axis=0, concat_axis=0, tiled=True)
    out_weight = out_weight + arrived[0, 0, 0, 0] * jnp.zeros((), out_weight.dtype)
    key_slots, unused_video = slot_masks(
        lengths, text_len, jnp.arange(slot_count, dtype=jnp.int32), capacity
    )
    bias = jnp.where(key_slots, 0.0, -jnp.inf).astype(jnp.float32)
    attended = attention(arrived, bias)
    returned = lax.all_to_all(
        attended.reshape(seq_count, capacity, group_width),
        "seq",
        split_axis=0,
        concat_axis=0,
        tiled=True,
    )
    cfg_index = lax.axis_index("cfg")
    weight_half = lax.all_gather(out_weight, "seq", axis=0, tiled=True)
    partner_rows = partner_2(returned, "cfg", 0)
    own_first = cfg_index == 0
    both = jnp.stack(
        [jnp.where(own_first, returned, partner_rows), jnp.where(own_first, partner_rows, returned)]
    )
    hidden = jnp.einsum(
        "agsj,gjc->asc",
        both,
        weight_half.reshape(seq_count, group_width, out_weight.shape[1]),
        preferred_element_type=jnp.float32,
    )
    half_width = out_weight.shape[1]
    column_start = cfg_index * half_width
    sums = jnp.stack([jnp.sum(hidden, axis=2), jnp.sum(hidden * hidden, axis=2)])
    sums = sums + partner_2(sums, "cfg", 0)
    row_mean = (sums[0] / D)[:, :, None]
    spread = (sums[1] / D)[:, :, None] - row_mean * row_mean
    shift_part = lax.dynamic_slice_in_dim(modulation[0, 0], column_start, half_width, 0)
    gain_part = lax.dynamic_slice_in_dim(modulation[0, 1], column_start, half_width, 0)
    normed = modulate(hidden, row_mean, spread, shift_part, gain_part)
    proj_half = lax.dynamic_slice_in_dim(proj_weight, column_start, half_width, 0)
    velocity = jnp.dot(
        normed.reshape(2 * capacity, half_width), proj_half, preferred_element_type=jnp.float32
    ).reshape(2, capacity, 2, OUT_CH // 2)
    own_half = jnp.where(own_first, velocity[:, :, 0], velocity[:, :, 1])
    other_half = jnp.where(own_first, velocity[:, :, 1], velocity[:, :, 0])
    velocity = own_half + partner_2(other_half, "cfg", 0)
    conditional = velocity[0][None]
    unconditional = velocity[1][None]
    own_slots = lax.axis_index("seq") * capacity + jnp.arange(capacity, dtype=jnp.int32)
    unused_keys, video_slots = slot_masks(lengths, text_len, own_slots, capacity)
    video_mask = video_slots[:, :, None]
    guided = jnp.where(video_mask, unconditional + guide_scale * (conditional - unconditional), 0.0)
    alpha_now, alpha_prev = plan(timestep)
    clean_part = jnp.sqrt(alpha_now) * latent - jnp.sqrt(1.0 - alpha_now) * guided
    noise_part = jnp.sqrt(1.0 - alpha_now) * latent + jnp.sqrt(alpha_now) * guided
    previous = jnp.where(
        video_mask, jnp.sqrt(alpha_prev) * clean_part + jnp.sqrt(1.0 - alpha_prev) * noise_part, 0.0
    )
    return (guided, previous)


def solution(mesh):
    placed = (
        P("cfg", "req", "seq", None),
        P("req", None),
        P("req"),
        P("seq", "cfg"),
        P("req", None, None),
        P(),
        P("req", "seq", "cfg"),
        P("req"),
    )
    return jax.shard_map(
        body,
        mesh=mesh,
        in_specs=placed,
        out_specs=(P("req", "seq", "cfg"), P("req", "seq", "cfg")),
        check_vma=False,
    )
```

```python
import math

import jax
import jax.numpy as jnp
from jax import lax
from jax.sharding import PartitionSpec as P
from jax.experimental import pallas as pl
from jax.experimental.pallas import tpu as pltpu

D = 3072
HEAD = 64
OUT_CH = 64
TEXT = 226


guide_scale = 6.0
ln_epsilon = 1e-05
step_gap = 20


def partner_2(array, axis, bit):
    return lax.ppermute(array, axis, [(i, i ^ 1 << bit) for i in range(lax.axis_size(axis))])


def slot_masks(lengths, text_len, slot_ids, capacity):
    piece_ids = slot_ids // capacity
    local_ids = slot_ids % capacity
    seq_ids = jnp.arange(lengths.shape[1], dtype=jnp.int32)
    select = (piece_ids[None, :] == seq_ids[:, None]).astype(jnp.int32)
    offsets = jnp.cumsum(lengths, axis=1) - lengths
    piece_len = jnp.sum(lengths[:, :, None] * select[None], axis=1)
    start_pos = jnp.sum(offsets[:, :, None] * select[None], axis=1)
    position = start_pos + local_ids[None, :]
    live_slots = local_ids[None, :] < piece_len
    key_slots = live_slots & ((position >= TEXT) | (position < text_len[:, None]))
    video_slots = live_slots & (position >= TEXT)
    return (key_slots, video_slots)


def plan(timestep):
    indices = jnp.arange(1000, dtype=jnp.int32)
    counter = jnp.arange(1000, dtype=jnp.float32)
    root_beta = math.sqrt(0.00085) + (math.sqrt(0.012) - math.sqrt(0.00085)) * counter / 999.0
    log_keep = jnp.log1p(-root_beta * root_beta)
    current = timestep[0]
    earlier = jnp.maximum(current - step_gap, 0)
    alpha_now = jnp.exp(jnp.sum(jnp.where(indices <= current, log_keep, 0.0)))
    alpha_prev = jnp.exp(jnp.sum(jnp.where(indices <= earlier, log_keep, 0.0)))
    return (alpha_now, alpha_prev)


def attention_kernel(q_ref, k_ref, v_ref, bias_ref, o_ref):
    query = q_ref[0, 0]
    slot_count = k_ref.shape[0] * k_ref.shape[2]
    keyset = k_ref[...].reshape(slot_count, k_ref.shape[3])
    values = v_ref[...].reshape(slot_count, v_ref.shape[3])
    bias = bias_ref[...]
    lane = lax.broadcasted_iota(jnp.int32, query.shape, 1)
    results = []
    for head in range(2):
        own = (lane >= HEAD) if head else (lane < HEAD)
        masked = jnp.where(own, query, jnp.zeros_like(query))
        scores = lax.dot_general(
            masked, keyset, (((1,), (1,)), ((), ())), preferred_element_type=jnp.float32
        )
        scores = scores * (1.0 / math.sqrt(HEAD)) + bias
        row_top = jnp.max(scores, axis=1, keepdims=True)
        weights = jnp.exp(scores - row_top)
        total = jnp.sum(weights, axis=1, keepdims=True)
        probs = (weights * (1.0 / total)).astype(jnp.bfloat16)
        results.append(jnp.dot(probs, values, preferred_element_type=jnp.float32))
    o_ref[...] = jnp.where(lane < HEAD, results[0], results[1]).astype(o_ref.dtype)


def attention(blocks, bias):
    piece_count, unused, capacity, width = blocks.shape
    whole = (piece_count, 1, capacity, width)
    return pl.pallas_call(
        attention_kernel,
        grid=(piece_count,),
        in_specs=[
            pl.BlockSpec((1, 1, capacity, width), lambda i: (i, 0, 0, 0)),
            pl.BlockSpec(whole, lambda i: (0, 1, 0, 0)),
            pl.BlockSpec(whole, lambda i: (0, 2, 0, 0)),
            pl.BlockSpec((1, piece_count * capacity), lambda i: (0, 0)),
        ],
        out_specs=pl.BlockSpec((capacity, width), lambda i: (i, 0)),
        out_shape=jax.ShapeDtypeStruct((piece_count * capacity, width), jnp.bfloat16),
        compiler_params=pltpu.CompilerParams(vmem_limit_bytes=48 * 1024 * 1024),
    )(blocks, blocks, blocks, bias)


def modulate(hidden, row_mean, spread, shift_part, gain_part):
    return (
        (hidden - row_mean) / jnp.sqrt(spread + ln_epsilon) * (1.0 + gain_part) + shift_part
    ).astype(jnp.bfloat16)


def body(projected, lengths, text_len, out_weight, modulation, proj_weight, latent, timestep):
    seq_count = lax.axis_size("seq")
    item_count, capacity = (projected.shape[1], projected.shape[2])
    attn_width = projected.shape[3] // 3
    group_width = attn_width // seq_count
    slot_count = capacity * seq_count
    outgoing = projected[0, 0].reshape(capacity, 3, seq_count, group_width)
    outgoing = outgoing.transpose(2, 1, 0, 3)
    arrived = lax.all_to_all(outgoing, "seq", split_axis=0, concat_axis=0, tiled=True)
    out_weight = out_weight + arrived[0, 0, 0, 0] * jnp.zeros((), out_weight.dtype)
    key_slots, unused_video = slot_masks(
        lengths, text_len, jnp.arange(slot_count, dtype=jnp.int32), capacity
    )
    bias = jnp.where(key_slots, 0.0, -jnp.inf).astype(jnp.float32)
    attended = attention(arrived, bias)
    returned = lax.all_to_all(
        attended.reshape(seq_count, capacity, group_width),
        "seq",
        split_axis=0,
        concat_axis=0,
        tiled=True,
    )
    cfg_index = lax.axis_index("cfg")
    weight_half = lax.all_gather(out_weight, "seq", axis=0, tiled=True)
    partner_rows = partner_2(returned, "cfg", 0)
    own_first = cfg_index == 0
    weight_rows = weight_half.reshape(seq_count, group_width, out_weight.shape[1])
    hidden = jnp.stack(
        [
            jnp.einsum("gsj,gjc->sc", rows, weight_rows, preferred_element_type=jnp.float32)
            for rows in (returned, partner_rows)
        ]
    )
    half_width = out_weight.shape[1]
    column_start = cfg_index * half_width
    sums = jnp.stack([jnp.sum(hidden, axis=2), jnp.sum(hidden * hidden, axis=2)])
    sums = sums + partner_2(sums, "cfg", 0)[:, ::-1]
    row_mean = (sums[0] / D)[:, :, None]
    spread = (sums[1] / D)[:, :, None] - row_mean * row_mean
    shift_part = lax.dynamic_slice_in_dim(modulation[0, 0], column_start, half_width, 0)
    gain_part = lax.dynamic_slice_in_dim(modulation[0, 1], column_start, half_width, 0)
    normed = modulate(hidden, row_mean, spread, shift_part, gain_part)
    proj_half = lax.dynamic_slice_in_dim(proj_weight, column_start, half_width, 0)
    velocity = jnp.dot(
        normed.reshape(2 * capacity, half_width), proj_half, preferred_element_type=jnp.float32
    ).reshape(2, capacity, 2, OUT_CH // 2)
    own_half = jnp.where(own_first, velocity[:, :, 0], velocity[:, :, 1])
    other_half = jnp.where(own_first, velocity[:, :, 1], velocity[:, :, 0])
    velocity = own_half + partner_2(other_half, "cfg", 0)[::-1]
    conditional = jnp.where(own_first, velocity[0], velocity[1])[None]
    unconditional = jnp.where(own_first, velocity[1], velocity[0])[None]
    own_slots = lax.axis_index("seq") * capacity + jnp.arange(capacity, dtype=jnp.int32)
    unused_keys, video_slots = slot_masks(lengths, text_len, own_slots, capacity)
    video_mask = video_slots[:, :, None]
    guided = jnp.where(video_mask, unconditional + guide_scale * (conditional - unconditional), 0.0)
    alpha_now, alpha_prev = plan(timestep)
    clean_part = jnp.sqrt(alpha_now) * latent - jnp.sqrt(1.0 - alpha_now) * guided
    noise_part = jnp.sqrt(1.0 - alpha_now) * latent + jnp.sqrt(alpha_now) * guided
    previous = jnp.where(
        video_mask, jnp.sqrt(alpha_prev) * clean_part + jnp.sqrt(1.0 - alpha_prev) * noise_part, 0.0
    )
    return (guided, previous)


def solution(mesh):
    placed = (
        P("cfg", "req", "seq", None),
        P("req", None),
        P("req"),
        P("seq", "cfg"),
        P("req", None, None),
        P(),
        P("req", "seq", "cfg"),
        P("req"),
    )
    return jax.shard_map(
        body,
        mesh=mesh,
        in_specs=placed,
        out_specs=(P("req", "seq", "cfg"), P("req", "seq", "cfg")),
        check_vma=False,
    )
```

```python
import math

import jax
import jax.numpy as jnp
from jax import lax
from jax.sharding import PartitionSpec as P
from jax.experimental import pallas as pl
from jax.experimental.pallas import tpu as pltpu

D = 3072
HEAD = 64
OUT_CH = 64
TEXT = 226


guide_scale = 6.0
ln_epsilon = 1e-05
step_gap = 20


def partner_2(array, axis, bit):
    return lax.ppermute(array, axis, [(i, i ^ 1 << bit) for i in range(lax.axis_size(axis))])


def slot_masks(lengths, text_len, slot_ids, capacity):
    piece_ids = slot_ids // capacity
    local_ids = slot_ids % capacity
    seq_ids = jnp.arange(lengths.shape[1], dtype=jnp.int32)
    select = (piece_ids[None, :] == seq_ids[:, None]).astype(jnp.int32)
    offsets = jnp.cumsum(lengths, axis=1) - lengths
    piece_len = jnp.sum(lengths[:, :, None] * select[None], axis=1)
    start_pos = jnp.sum(offsets[:, :, None] * select[None], axis=1)
    position = start_pos + local_ids[None, :]
    live_slots = local_ids[None, :] < piece_len
    key_slots = live_slots & ((position >= TEXT) | (position < text_len[:, None]))
    video_slots = live_slots & (position >= TEXT)
    return (key_slots, video_slots)


def plan(timestep):
    indices = jnp.arange(1000, dtype=jnp.int32)
    counter = jnp.arange(1000, dtype=jnp.float32)
    root_beta = math.sqrt(0.00085) + (math.sqrt(0.012) - math.sqrt(0.00085)) * counter / 999.0
    log_keep = jnp.log1p(-root_beta * root_beta)
    current = timestep[0]
    earlier = jnp.maximum(current - step_gap, 0)
    limits = jnp.stack([current, earlier])[:, None]
    alphas = jnp.exp(jnp.sum(jnp.where(indices[None, :] <= limits, log_keep[None, :], 0.0), axis=1))
    return (alphas[0], alphas[1])


def attention_kernel(q_ref, k_ref, v_ref, bias_ref, o_ref):
    query = q_ref[0, 0]
    slot_count = k_ref.shape[0] * k_ref.shape[2]
    keyset = k_ref[...].reshape(slot_count, k_ref.shape[3])
    values = v_ref[...].reshape(slot_count, v_ref.shape[3])
    bias = bias_ref[...]
    lane = lax.broadcasted_iota(jnp.int32, query.shape, 1)
    results = []
    for head in range(2):
        own = (lane >= HEAD) if head else (lane < HEAD)
        masked = jnp.where(own, query, jnp.zeros_like(query))
        scores = lax.dot_general(
            masked, keyset, (((1,), (1,)), ((), ())), preferred_element_type=jnp.float32
        )
        scores = scores * (1.0 / math.sqrt(HEAD)) + bias
        row_top = jnp.max(scores, axis=1, keepdims=True)
        weights = jnp.exp(scores - row_top)
        total = jnp.sum(weights, axis=1, keepdims=True)
        probs = (weights * (1.0 / total)).astype(jnp.bfloat16)
        results.append(jnp.dot(probs, values, preferred_element_type=jnp.float32))
    o_ref[...] = jnp.where(lane < HEAD, results[0], results[1]).astype(o_ref.dtype)


def attention(blocks, bias):
    piece_count, unused, capacity, width = blocks.shape
    whole = (piece_count, 1, capacity, width)
    return pl.pallas_call(
        attention_kernel,
        grid=(piece_count,),
        in_specs=[
            pl.BlockSpec((1, 1, capacity, width), lambda i: (i, 0, 0, 0)),
            pl.BlockSpec(whole, lambda i: (0, 1, 0, 0)),
            pl.BlockSpec(whole, lambda i: (0, 2, 0, 0)),
            pl.BlockSpec((1, piece_count * capacity), lambda i: (0, 0)),
        ],
        out_specs=pl.BlockSpec((capacity, width), lambda i: (i, 0)),
        out_shape=jax.ShapeDtypeStruct((piece_count * capacity, width), jnp.bfloat16),
        compiler_params=pltpu.CompilerParams(vmem_limit_bytes=48 * 1024 * 1024),
    )(blocks, blocks, blocks, bias)


def modulate(hidden, row_mean, spread, shift_part, gain_part):
    return (
        (hidden - row_mean) / jnp.sqrt(spread + ln_epsilon) * (1.0 + gain_part) + shift_part
    ).astype(jnp.bfloat16)


def body(projected, lengths, text_len, out_weight, modulation, proj_weight, latent, timestep):
    seq_count = lax.axis_size("seq")
    item_count, capacity = (projected.shape[1], projected.shape[2])
    attn_width = projected.shape[3] // 3
    group_width = attn_width // seq_count
    slot_count = capacity * seq_count
    outgoing = projected[0, 0].reshape(capacity, 3, seq_count, group_width)
    outgoing = outgoing.transpose(2, 1, 0, 3)
    arrived = lax.all_to_all(outgoing, "seq", split_axis=0, concat_axis=0, tiled=True)
    out_weight = out_weight + arrived[0, 0, 0, 0] * jnp.zeros((), out_weight.dtype)
    key_slots, unused_video = slot_masks(
        lengths, text_len, jnp.arange(slot_count, dtype=jnp.int32), capacity
    )
    bias = jnp.where(key_slots, 0.0, -jnp.inf).astype(jnp.float32)
    attended = attention(arrived, bias)
    returned = lax.all_to_all(
        attended.reshape(seq_count, capacity, group_width),
        "seq",
        split_axis=0,
        concat_axis=0,
        tiled=True,
    )
    cfg_index = lax.axis_index("cfg")
    weight_half = lax.all_gather(out_weight, "seq", axis=0, tiled=True)
    partner_rows = partner_2(returned, "cfg", 0)
    own_first = cfg_index == 0
    weight_rows = weight_half.reshape(seq_count, group_width, out_weight.shape[1])
    hidden = jnp.stack(
        [
            jnp.einsum("gsj,gjc->sc", rows, weight_rows, preferred_element_type=jnp.float32)
            for rows in (returned, partner_rows)
        ]
    )
    half_width = out_weight.shape[1]
    column_start = cfg_index * half_width
    sums = jnp.stack([jnp.sum(hidden, axis=2), jnp.sum(hidden * hidden, axis=2)])
    sums = sums + partner_2(sums, "cfg", 0)[:, ::-1]
    row_mean = (sums[0] / D)[:, :, None]
    spread = (sums[1] / D)[:, :, None] - row_mean * row_mean
    shift_part = lax.dynamic_slice_in_dim(modulation[0, 0], column_start, half_width, 0)
    gain_part = lax.dynamic_slice_in_dim(modulation[0, 1], column_start, half_width, 0)
    normed = modulate(hidden, row_mean, spread, shift_part, gain_part)
    proj_half = lax.dynamic_slice_in_dim(proj_weight, column_start, half_width, 0)
    velocity = jnp.dot(
        normed.reshape(2 * capacity, half_width), proj_half, preferred_element_type=jnp.float32
    ).reshape(2, capacity, 2, OUT_CH // 2)
    own_half = jnp.where(own_first, velocity[:, :, 0], velocity[:, :, 1])
    other_half = jnp.where(own_first, velocity[:, :, 1], velocity[:, :, 0])
    velocity = own_half + partner_2(other_half, "cfg", 0)[::-1]
    conditional = jnp.where(own_first, velocity[0], velocity[1])[None]
    unconditional = jnp.where(own_first, velocity[1], velocity[0])[None]
    own_slots = lax.axis_index("seq") * capacity + jnp.arange(capacity, dtype=jnp.int32)
    unused_keys, video_slots = slot_masks(lengths, text_len, own_slots, capacity)
    video_mask = video_slots[:, :, None]
    guided = jnp.where(video_mask, unconditional + guide_scale * (conditional - unconditional), 0.0)
    alpha_now, alpha_prev = plan(timestep)
    clean_part = jnp.sqrt(alpha_now) * latent - jnp.sqrt(1.0 - alpha_now) * guided
    noise_part = jnp.sqrt(1.0 - alpha_now) * latent + jnp.sqrt(alpha_now) * guided
    previous = jnp.where(
        video_mask, jnp.sqrt(alpha_prev) * clean_part + jnp.sqrt(1.0 - alpha_prev) * noise_part, 0.0
    )
    return (guided, previous)


def solution(mesh):
    placed = (
        P("cfg", "req", "seq", None),
        P("req", None),
        P("req"),
        P("seq", "cfg"),
        P("req", None, None),
        P(),
        P("req", "seq", "cfg"),
        P("req"),
    )
    return jax.shard_map(
        body,
        mesh=mesh,
        in_specs=placed,
        out_specs=(P("req", "seq", "cfg"), P("req", "seq", "cfg")),
        check_vma=False,
    )
```
